128 devices in a mesh: leaf: 32 (over z, y, core), blk: 4 (over x).
Axes of the slice: x: 4, y: 4, z: 4, core: 2. Of those that a mesh axis runs over, the one named last changes fastest.
Arguments:
- panels: float32 [4, 262144], P(None, ('leaf', 'blk')), may hold values from 0 to 10, as said below
- panel_dest: int32 [262144, 1], P(('leaf', 'blk')), may hold values from 0 to 127; in each aligned block of 2048 rows (0 to 2047, 2048 to 4095, ...) at most 32 rows name the same one
- proxy_pool: float32 [3, 8192], replicated, may hold values from -0.5 to 1.5
- proxy_index: int32 [32, 2048], P('leaf'), may hold values from 0 to 8191
- omega: bfloat16 [32, 2048, 128], P('leaf', 'blk'), may hold values from -0.125 to 0.125
- merge_maps: float32 [62, 128, 128], replicated, may hold values from -0.5 to 0.5
Outputs:
- leaf_basis: float32 [128, 262144], P(None, ('leaf', 'blk'))
- leaf_factor: float32 [32, 128, 128], P('leaf')
- ancestor_factor: float32 [32, 5, 128, 128], P('leaf')
The draws below stay inside these ranges and needn't reach their ends.
Inputs may be any that keep to these rules, and one draw needn't show every extreme that they name: panel_dest holds device numbers, leaf index times 4 plus blk index; of the 2048 panels of one device at most 32 go to the same device, and that many do in some device's panels. `panels`: rows 0 to 2 are coordinates in the unit cube, row 3 a positive weight.
All inputs are finite; a program needn't handle non-finite values.
Results may differ from the reference program's by a relative error of at most 0.012.
The reference program's roundings to bfloat16 on the way count: a program that leaves them out, or rounds other values in their place, can miss the bound.
Values may be sent and summed in bfloat16 or wider, within the bound.
No kernel may reach another device: no remote copies, remote signals or barrier semaphores. Data moves between devices by JAX's collectives and lax.ppermute only.
A program may use at most 64 MiB of HBM per device.

```python
import math
import jax
import jax.numpy as jnp
import numpy as np
from jax import lax

P_DEV = 2048
NPROXY = 2048
RANK = 128
POOL = 8192
CAP = 32
PANELS = 262144
NODES = 62
N_LEAF = 32
N_BLK = 4
DEVICES = 128


def draw_panels(key, part):
    coord_key = jax.random.fold_in(key, 11)
    weight_key = jax.random.fold_in(key, 12)
    coords = jax.random.uniform(coord_key, (3, PANELS), jnp.float32)
    log_weight = jax.random.uniform(weight_key, (1, PANELS), jnp.float32, minval=math.log(0.3), maxval=math.log(3.0))
    return jnp.concatenate([coords, jnp.exp(log_weight)], axis=0)


def place_ends(array, rng, smallest, top_value):
    dims = array.shape
    index_at = [jax.random.randint(jax.random.fold_in(rng, axis), (), 0, dims[axis]) for axis in range(len(dims))]
    array = array.at[tuple(index_at)].set(smallest)
    longest = dims.index(max(dims))
    index_at[longest] = (index_at[longest] + 1) % dims[longest]
    return array.at[tuple(index_at)].set(top_value)


def block_levels(own_key, extent, cuts, low, high):
    factor_of, own = 1.0, jax.random.fold_in(own_key, 6)
    for dim, parts in cuts:
        steps = jnp.exp(jax.random.uniform(jax.random.fold_in(own, dim), (parts,), jnp.float32, low / len(cuts), high / len(cuts)))
        factor_of = factor_of * jnp.repeat(steps, extent[dim] // parts).reshape([-1 if axis == dim else 1 for axis in range(len(extent))])
    return factor_of


def deal_out(key, own, number, rows, amount, top, most, lean):
    sequence = jax.random.permutation(key, amount)
    packed, ordinary = load_shares(amount, rows * top, most, lean, True), load_shares(amount, rows * top, most, lean, False)
    places = jnp.arange(amount)

    def named(tallies, turn):
        used = int((tallies > 0).sum())
        fixed = max(1, used // 4)
        moved = fixed + (places - fixed + turn * (used - fixed)) % max(1, amount - fixed)
        return jnp.zeros((amount,), jnp.int32).at[sequence[jnp.where(places < fixed, places, moved)]].set(jnp.asarray(tallies, jnp.int32))

    tallies = jnp.where(number % 4 == 0, named(packed, number // 4), named(ordinary, number - number // 4 - 1))
    mixed = jax.random.permutation(jax.random.fold_in(own, 3), amount)
    source_of, receiver = mixed[0:amount // 2 * 2:2], mixed[1:amount // 2 * 2:2]
    margin = jnp.minimum(tallies[source_of] - 1, most - tallies[receiver]) // 2
    margin = jnp.where((source_of == sequence[0]) | (receiver == sequence[0]) | (tallies[receiver] == 0), 0, jnp.maximum(margin, 0))
    moved = jax.random.randint(jax.random.fold_in(own, 4), (amount // 2,), 0, 1 << 20) % (margin + 1)
    tallies = tallies.at[source_of].add(-moved).at[receiver].add(moved)
    members = jnp.searchsorted(jnp.cumsum(tallies), jnp.arange(rows * top), side="right").astype(jnp.int32)
    grid = members.reshape(top, rows).T
    grid = grid[jax.random.permutation(jax.random.fold_in(own, 1), rows)]
    turn = jax.random.randint(jax.random.fold_in(own, 2), (rows, 1), 0, top)
    return jnp.take_along_axis(grid, (jnp.arange(top)[None, :] + turn) % top, axis=1)


def load_shares(number_of, total, limit, slope, full):
    loads = [(1 << 20) // math.isqrt(rank ** slope) + 1 for rank in range(1, number_of + 1)]
    largest = limit if full else min(limit, max(-(-total // number_of), total * loads[0] // sum(loads)))
    least = 1 if total - largest >= number_of - 1 else 0
    holding, spare = [largest] + [least] * (number_of - 1), total - largest - least * (number_of - 1)
    while spare > 0:
        free = [i for i in range(1, number_of) if holding[i] < largest] or [i for i in range(1, number_of) if holding[i] < limit]
        whole, budget = sum([loads[i] for i in free]), spare
        for i in free:
            addition = min(limit - holding[i], max(1, budget * loads[i] // whole), spare)
            holding[i] = holding[i] + addition
            spare = spare - addition
    return np.array(holding)


def gaussian(key, extent, spread, reach, pieces=(), kind=jnp.bfloat16):
    drawn = spread * jax.random.normal(key, extent, jnp.float32)
    if pieces:
        drawn = drawn * block_levels(key, extent, pieces, -0.22, 0.18)
    return jnp.clip(drawn, -reach, reach).astype(kind)


def setup_inputs(seed: int = 0) -> dict:
    seeds = jax.random.split(jax.random.key(seed), 7)
    panels = draw_panels(jax.random.fold_in(seeds[6], 71), 0)
    panel_dest_keys = jax.random.split(jax.random.fold_in(seeds[1], 1), PANELS // P_DEV)
    panel_dest_turns = jax.random.permutation(jax.random.fold_in(seeds[1], 3), PANELS // P_DEV)
    panel_dest = jax.vmap(lambda own, number: deal_out(jax.random.fold_in(seeds[1], 2), own, number, P_DEV, DEVICES, 1, CAP, 2))(panel_dest_keys, panel_dest_turns).reshape((PANELS, 1))
    proxy_pool = jnp.clip(jax.random.uniform(seeds[2], (3, POOL), jnp.float32, -0.5, 1.5), -0.5, 1.5)
    proxy_index = place_ends(jax.random.randint(seeds[3], (N_LEAF, NPROXY), 0, POOL), jax.random.fold_in(seeds[3], 1), 0, POOL - 1).astype(jnp.int32)
    omega = gaussian(seeds[4], (N_LEAF, NPROXY, RANK), NPROXY ** -0.5, 0.125, ((0, 32), (1, 4)))
    merge_maps = gaussian(seeds[5], (NODES, RANK, RANK), RANK ** -0.5, 0.5, (), jnp.float32)
    return dict(panels=panels, panel_dest=panel_dest, proxy_pool=proxy_pool, proxy_index=proxy_index, omega=omega, merge_maps=merge_maps)


def kernel_tile(row_data, points):
    delta_x = row_data[0][:, None] - points[0][None, :]
    delta_y = row_data[1][:, None] - points[1][None, :]
    delta_z = row_data[2][:, None] - points[2][None, :]
    distance = delta_x * delta_x + delta_y * delta_y + delta_z * delta_z
    return (row_data[3][:, None] * lax.rsqrt(distance + 0.0009)).astype(jnp.bfloat16)

def reference(panels, panel_dest, proxy_pool, proxy_index, omega, merge_maps):
    block_rows = 512
    highest = lax.Precision.HIGHEST
    panel_total = panels.shape[1]
    rank_width = omega.shape[2]
    identity = jnp.eye(rank_width, dtype=jnp.float32)
    leaf_of = (panel_dest[:, 0] // N_BLK).astype(jnp.int32)
    ordering = jnp.argsort(leaf_of, stable=True).astype(jnp.int32)
    leaf_counts = jnp.zeros((N_LEAF,), jnp.int32).at[leaf_of].add(1)
    leaf_stops = jnp.cumsum(leaf_counts).astype(jnp.int32)
    leaf_starts = (leaf_stops - leaf_counts).astype(jnp.int32)
    ordered = jnp.concatenate([panels[:, ordering], jnp.zeros((4, block_rows), panels.dtype)], axis=1)
    store_init = jnp.zeros((panel_total + block_rows, rank_width), jnp.float32)
    grams_init = jnp.zeros((N_LEAF, rank_width, rank_width), jnp.float32)
    factors_init = jnp.zeros((N_LEAF, rank_width, rank_width), jnp.float32)

    def one_leaf(leaf_index, carry):
        sketch_store, grams, factors = carry
        points = jnp.take(proxy_pool, proxy_index[leaf_index], axis=1)
        sketch_map = omega[leaf_index]
        start_row = leaf_starts[leaf_index]
        stop_row = leaf_stops[leaf_index]
        block_count = (stop_row - start_row + block_rows - 1) // block_rows

        def rows_of(step_index):
            first_row = (start_row + step_index * block_rows).astype(jnp.int32)
            live_rows = first_row + jnp.arange(block_rows, dtype=jnp.int32) < stop_row
            return (first_row, live_rows)

        def sketch_block(step_index, state):
            store_now, gram_sum = state
            first_row, live_rows = rows_of(step_index)
            row_data = lax.dynamic_slice_in_dim(ordered, first_row, block_rows, 1)
            row_data = row_data * live_rows.astype(row_data.dtype)[None, :]
            tile = kernel_tile(row_data, points)
            sketch = jnp.dot(tile.astype(jnp.float32), sketch_map.astype(jnp.float32), preferred_element_type=jnp.float32)
            gram_sum = gram_sum + jnp.dot(sketch.T, sketch, precision=highest)
            previous = lax.dynamic_slice_in_dim(store_now, first_row, block_rows, 0)
            store_now = lax.dynamic_update_slice_in_dim(store_now, jnp.where(live_rows[:, None], sketch, previous), first_row, 0)
            return (store_now, gram_sum)
        sketch_store, gram_sum = lax.fori_loop(0, block_count, sketch_block, (sketch_store, jnp.zeros((rank_width, rank_width), jnp.float32)))
        gram_full = gram_sum / (P_DEV * N_BLK) + identity
        lower_factor = jnp.linalg.cholesky(gram_full)

        def solve_block(step_index, store_now):
            first_row, live_rows = rows_of(step_index)
            previous = lax.dynamic_slice_in_dim(store_now, first_row, block_rows, 0)
            solved = jax.scipy.linalg.solve_triangular(lower_factor, previous.T, lower=True).T
            return lax.dynamic_update_slice_in_dim(store_now, jnp.where(live_rows[:, None], solved, previous), first_row, 0)
        sketch_store = lax.fori_loop(0, block_count, solve_block, sketch_store)
        return (sketch_store, grams.at[leaf_index].set(gram_full), factors.at[leaf_index].set(lower_factor))
    sketch_store, grams, factors = lax.fori_loop(0, N_LEAF, one_leaf, (store_init, grams_init, factors_init))
    leaf_basis = jnp.zeros((rank_width, panel_total), jnp.float32).at[:, ordering].set(sketch_store[:panel_total].T)
    levels = int(N_LEAF).bit_length() - 1
    leaf_ids = jnp.arange(N_LEAF, dtype=jnp.int32)
    node_gram = grams
    per_level = []
    for level_index in range(levels):
        node_count = N_LEAF >> level_index
        level_maps = merge_maps[node_count - 2:2 * node_count - 2]
        level_terms = jnp.matmul(jnp.matmul(jnp.swapaxes(level_maps, 1, 2), node_gram, precision=highest), level_maps, precision=highest)
        node_gram = (level_terms[0::2] + level_terms[1::2]) * 0.5
        level_factors = jnp.linalg.cholesky(node_gram)
        per_level.append(level_factors[leaf_ids >> level_index + 1])
    ancestor_factor = jnp.stack(per_level, axis=1)
    return (leaf_basis, factors, ancestor_factor)
```

```python
import functools

import jax
import jax.numpy as jnp
from jax import lax
from jax.experimental import pallas as pl
from jax.experimental.pallas import tpu as pltpu
from jax.sharding import PartitionSpec as P


def from_partner(value, axis, bit):
    mask = 2**bit
    pairs = [(source, source ^ mask) for source in range(lax.axis_size(axis))]
    return lax.ppermute(value, axis, pairs)


def from_shift(value, axis, shift):
    size = lax.axis_size(axis)
    pairs = [(source, (source + shift) % size) for source in range(size)]
    return lax.ppermute(value, axis, pairs)


def kernel_tile(row_data, points):
    delta_x = row_data[0][:, None] - points[0][None, :]
    delta_y = row_data[1][:, None] - points[1][None, :]
    delta_z = row_data[2][:, None] - points[2][None, :]
    distance = delta_x * delta_x + delta_y * delta_y + delta_z * delta_z
    return (row_data[3][:, None] * lax.rsqrt(distance + 0.0009)).astype(jnp.bfloat16)


def _cholesky_body(with_inverse, a_ref, l_ref, *rest):
    if with_inverse:
        inv_ref, work, inverse_work = rest
    else:
        (work,) = rest
    count, n, _ = a_ref.shape
    rows = lax.broadcasted_iota(jnp.int32, (n, n), 0)
    cols = lax.broadcasted_iota(jnp.int32, (n, n), 1)
    sub = lax.broadcasted_iota(jnp.int32, (n, 1), 0)
    lane = lax.broadcasted_iota(jnp.int32, (1, n), 1)
    work[...] = a_ref[...]
    if with_inverse:
        eye = jnp.where(rows == cols, 1.0, 0.0).astype(jnp.float32)
        for b in range(count):
            inverse_work[b] = eye

    def step(j, carry):
        for b in range(count):
            full = work[b]
            row = work[b, pl.ds(j, 1), :]
            pivot = jnp.sum(jnp.where(lane == j, row, 0.0), axis=1, keepdims=True)
            scale = lax.rsqrt(pivot)
            column = jnp.sum(jnp.where(cols == j, full, 0.0), axis=1, keepdims=True)
            factor = jnp.where(sub > j, column / pivot, 0.0)
            work[b] = jnp.where(sub == j, row * scale, full - factor * row)
            if with_inverse:
                inverse_full = inverse_work[b]
                inverse_row = inverse_work[b, pl.ds(j, 1), :]
                inverse_work[b] = jnp.where(
                    sub == j, inverse_row * scale, inverse_full - factor * inverse_row
                )
        return carry

    lax.fori_loop(0, n, step, 0)
    for b in range(count):
        l_ref[b] = jnp.transpose(jnp.where(cols >= rows, work[b], 0.0))
        if with_inverse:
            inv_ref[b] = jnp.where(cols <= rows, inverse_work[b], 0.0)


def cholesky_batch(a, with_inverse):
    count, n, _ = a.shape
    shape = jax.ShapeDtypeStruct((count, n, n), jnp.float32)
    vmem = pl.BlockSpec(memory_space=pltpu.VMEM)
    scratch = [pltpu.VMEM((count, n, n), jnp.float32)] * (2 if with_inverse else 1)
    return pl.pallas_call(
        functools.partial(_cholesky_body, with_inverse),
        out_shape=(shape, shape) if with_inverse else shape,
        in_specs=[vmem],
        out_specs=(vmem, vmem) if with_inverse else vmem,
        scratch_shapes=scratch,
    )(a)


def per_device(panels, panel_dest, proxy_pool, proxy_index, omega, merge_maps):
    highest = lax.Precision.HIGHEST
    device_count = lax.axis_size(("leaf", "blk"))
    blk_count = lax.axis_size("blk")
    leaf_count = lax.axis_size("leaf")
    blk_index = lax.axis_index("blk")
    own_panels = panels.shape[1]
    capacity = 2 * own_panels // device_count
    rank_width = omega.shape[2]
    identity = jnp.eye(rank_width, dtype=jnp.float32)
    omega_parts = [omega[0]] + [from_shift(omega[0], "blk", shift) for shift in range(1, blk_count)]
    destination = panel_dest[:, 0]
    one_hot = (destination[:, None] == jnp.arange(device_count, dtype=jnp.int32)[None, :]).astype(
        jnp.int32
    )
    running = jnp.cumsum(one_hot, axis=0)
    slot_index = jnp.sum(running * one_hot, axis=1) - 1
    position = destination * capacity + slot_index
    outgoing = jnp.zeros((4, device_count * capacity), jnp.float32).at[:, position].set(panels)
    received = lax.all_to_all(outgoing, ("leaf", "blk"), split_axis=1, concat_axis=1, tiled=True)
    leaf_proxies = proxy_index[0]
    points = jnp.take(proxy_pool, leaf_proxies, axis=1)
    tile = kernel_tile(received, points)
    chunk = omega.shape[1]
    sketch = jnp.zeros((received.shape[1], rank_width), jnp.float32)
    for shift in range(blk_count):
        source = (blk_index - shift) % blk_count
        part = lax.dynamic_slice_in_dim(tile, source * chunk, chunk, 1)
        sketch = sketch + jnp.dot(part, omega_parts[shift], preferred_element_type=jnp.float32)
    gram_part = jnp.dot(sketch.T, sketch, precision=highest)
    gram_sum = gram_part + from_partner(gram_part, "blk", 0)
    gram_sum = gram_sum + from_partner(gram_sum, "blk", 1)
    gram_full = gram_sum / (own_panels * blk_count) + identity
    lower_factor, lower_inverse = cholesky_batch(gram_full[None], True)
    basis_rows = jnp.dot(lower_inverse[0], sketch.T, precision=highest)
    returned = lax.all_to_all(
        basis_rows.astype(jnp.bfloat16), ("leaf", "blk"), split_axis=1, concat_axis=1, tiled=True
    )
    leaf_basis = jnp.take(returned, position, axis=1).astype(jnp.float32)
    leaf_index = lax.axis_index("leaf")
    levels = leaf_count.bit_length() - 1
    node_gram = gram_full
    ancestors = []
    for level_index in range(levels):
        heap_index = (leaf_count >> level_index) + (leaf_index >> level_index)
        node_map = lax.dynamic_index_in_dim(merge_maps, heap_index - 2, 0, keepdims=False)
        own_term = jnp.dot(
            jnp.dot(node_map.T, node_gram, precision=highest), node_map, precision=highest
        )
        sibling = from_partner(own_term, "leaf", level_index)
        node_gram = (own_term + sibling) * 0.5
        ancestors.append(node_gram)
    ancestor_grams = jnp.stack(ancestors, axis=0)
    ancestor_factor = cholesky_batch(ancestor_grams, False)
    return (leaf_basis, lower_factor, ancestor_factor[None])


def solution(mesh):
    placed = (
        P(None, ("leaf", "blk")),
        P(("leaf", "blk"), None),
        P(),
        P("leaf", None),
        P("leaf", "blk", None),
        P(),
    )
    return jax.shard_map(
        per_device,
        mesh=mesh,
        in_specs=placed,
        out_specs=(P(None, ("leaf", "blk")), P("leaf", None, None), P("leaf", None, None, None)),
        check_vma=False,
    )
```

```python
import functools

import jax
import jax.numpy as jnp
from jax import lax
from jax.experimental import pallas as pl
from jax.experimental.pallas import tpu as pltpu
from jax.sharding import PartitionSpec as P


def from_partner(value, axis, bit):
    mask = 2**bit
    pairs = [(source, source ^ mask) for source in range(lax.axis_size(axis))]
    return lax.ppermute(value, axis, pairs)


def from_shift(value, axis, shift):
    size = lax.axis_size(axis)
    pairs = [(source, (source + shift) % size) for source in range(size)]
    return lax.ppermute(value, axis, pairs)


def kernel_tile(row_data, points):
    delta_x = row_data[0][:, None] - points[0][None, :]
    delta_y = row_data[1][:, None] - points[1][None, :]
    delta_z = row_data[2][:, None] - points[2][None, :]
    distance = delta_x * delta_x + delta_y * delta_y + delta_z * delta_z
    return (row_data[3][:, None] * lax.rsqrt(distance + 0.0009)).astype(jnp.bfloat16)


def _cholesky_body(with_inverse, a_ref, l_ref, *rest):
    if with_inverse:
        inv_ref, work, inverse_work = rest
    else:
        (work,) = rest
    count, n, _ = a_ref.shape
    rows = lax.broadcasted_iota(jnp.int32, (n, n), 0)
    cols = lax.broadcasted_iota(jnp.int32, (n, n), 1)
    work[...] = a_ref[...]
    if with_inverse:
        eye = jnp.where(rows == cols, 1.0, 0.0).astype(jnp.float32)
        for b in range(count):
            inverse_work[b] = eye
    for j in range(n):
        top = (j // 8) * 8
        sub = lax.broadcasted_iota(jnp.int32, (n - top, 1), 0) + top
        for b in range(count):
            block = work[b, top:, :]
            row = work[b, j:j + 1, :]
            pivot = row[:, j:j + 1]
            scale = lax.rsqrt(pivot)
            factor = jnp.where(sub > j, block[:, j:j + 1] * (1.0 / pivot), 0.0)
            work[b, top:, :] = jnp.where(sub == j, row * scale, block - factor * row)
            if with_inverse:
                inverse_block = inverse_work[b, top:, :]
                inverse_row = inverse_work[b, j:j + 1, :]
                inverse_work[b, top:, :] = jnp.where(
                    sub == j, inverse_row * scale, inverse_block - factor * inverse_row
                )
    for b in range(count):
        l_ref[b] = jnp.transpose(jnp.where(cols >= rows, work[b], 0.0))
        if with_inverse:
            inv_ref[b] = jnp.where(cols <= rows, inverse_work[b], 0.0)


def cholesky_batch(a, with_inverse):
    count, n, _ = a.shape
    shape = jax.ShapeDtypeStruct((count, n, n), jnp.float32)
    vmem = pl.BlockSpec(memory_space=pltpu.VMEM)
    scratch = [pltpu.VMEM((count, n, n), jnp.float32)] * (2 if with_inverse else 1)
    return pl.pallas_call(
        functools.partial(_cholesky_body, with_inverse),
        out_shape=(shape, shape) if with_inverse else shape,
        in_specs=[vmem],
        out_specs=(vmem, vmem) if with_inverse else vmem,
        scratch_shapes=scratch,
    )(a)


def per_device(panels, panel_dest, proxy_pool, proxy_index, omega, merge_maps):
    highest = lax.Precision.HIGHEST
    device_count = lax.axis_size(("leaf", "blk"))
    blk_count = lax.axis_size("blk")
    leaf_count = lax.axis_size("leaf")
    blk_index = lax.axis_index("blk")
    own_panels = panels.shape[1]
    capacity = 2 * own_panels // device_count
    rank_width = omega.shape[2]
    identity = jnp.eye(rank_width, dtype=jnp.float32)
    omega_parts = [omega[0]] + [from_shift(omega[0], "blk", shift) for shift in range(1, blk_count)]
    destination = panel_dest[:, 0]
    one_hot = (destination[:, None] == jnp.arange(device_count, dtype=jnp.int32)[None, :]).astype(
        jnp.int32
    )
    running = jnp.cumsum(one_hot, axis=0)
    slot_index = jnp.sum(running * one_hot, axis=1) - 1
    position = destination * capacity + slot_index
    outgoing = jnp.zeros((4, device_count * capacity), jnp.float32).at[:, position].set(panels)
    received = lax.all_to_all(outgoing, ("leaf", "blk"), split_axis=1, concat_axis=1, tiled=True)
    chunk = omega.shape[1]
    leaf_proxies = jnp.concatenate(
        [
            lax.dynamic_slice_in_dim(proxy_index[0], ((blk_index - shift) % blk_count) * chunk, chunk)
            for shift in range(blk_count)
        ]
    )
    points = jnp.take(proxy_pool, leaf_proxies, axis=1)
    tile = kernel_tile(received, points)
    sketch = jnp.dot(tile, jnp.concatenate(omega_parts, axis=0), preferred_element_type=jnp.float32)
    gram_part = jnp.dot(sketch.T, sketch, precision=highest)
    gram_sum = gram_part + from_partner(gram_part, "blk", 0)
    gram_sum = gram_sum + from_partner(gram_sum, "blk", 1)
    gram_full = gram_sum / (own_panels * blk_count) + identity
    lower_factor, lower_inverse = cholesky_batch(gram_full[None], True)
    basis_rows = jnp.dot(lower_inverse[0], sketch.T, precision=highest)
    returned = lax.all_to_all(
        basis_rows.astype(jnp.bfloat16), ("leaf", "blk"), split_axis=1, concat_axis=1, tiled=True
    )
    leaf_basis = jnp.take(returned, position, axis=1).astype(jnp.float32)
    leaf_index = lax.axis_index("leaf")
    levels = leaf_count.bit_length() - 1
    node_gram = gram_full
    ancestors = []
    for level_index in range(levels):
        heap_index = (leaf_count >> level_index) + (leaf_index >> level_index)
        node_map = lax.dynamic_index_in_dim(merge_maps, heap_index - 2, 0, keepdims=False)
        own_term = jnp.dot(
            jnp.dot(node_map.T, node_gram, precision=highest), node_map, precision=highest
        )
        sibling = from_partner(own_term, "leaf", level_index)
        node_gram = (own_term + sibling) * 0.5
        ancestors.append(node_gram)
    ancestor_grams = jnp.stack(ancestors, axis=0)
    ancestor_factor = cholesky_batch(ancestor_grams, False)
    return (leaf_basis, lower_factor, ancestor_factor[None])


def solution(mesh):
    placed = (
        P(None, ("leaf", "blk")),
        P(("leaf", "blk"), None),
        P(),
        P("leaf", None),
        P("leaf", "blk", None),
        P(),
    )
    return jax.shard_map(
        per_device,
        mesh=mesh,
        in_specs=placed,
        out_specs=(P(None, ("leaf", "blk")), P("leaf", None, None), P("leaf", None, None, None)),
        check_vma=False,
    )
```

```python
import functools

import jax
import jax.numpy as jnp
from jax import lax
from jax.experimental import pallas as pl
from jax.experimental.pallas import tpu as pltpu
from jax.sharding import PartitionSpec as P


def from_partner(value, axis, bit):
    mask = 2**bit
    pairs = [(source, source ^ mask) for source in range(lax.axis_size(axis))]
    return lax.ppermute(value, axis, pairs)


def from_shift(value, axis, shift):
    size = lax.axis_size(axis)
    pairs = [(source, (source + shift) % size) for source in range(size)]
    return lax.ppermute(value, axis, pairs)


def kernel_tile(row_data, points):
    delta_x = row_data[0][:, None] - points[0][None, :]
    delta_y = row_data[1][:, None] - points[1][None, :]
    delta_z = row_data[2][:, None] - points[2][None, :]
    distance = delta_x * delta_x + delta_y * delta_y + delta_z * delta_z
    return (row_data[3][:, None] * lax.rsqrt(distance + 0.0009)).astype(jnp.bfloat16)


def _cholesky_body(with_inverse, a_ref, l_ref, *rest):
    if with_inverse:
        inv_ref, work, inverse_work = rest
    else:
        (work,) = rest
    count, n, _ = a_ref.shape
    rows = lax.broadcasted_iota(jnp.int32, (n, n), 0)
    cols = lax.broadcasted_iota(jnp.int32, (n, n), 1)
    work[...] = a_ref[...]
    if with_inverse:
        eye = jnp.where(rows == cols, 1.0, 0.0).astype(jnp.float32)
        for b in range(count):
            inverse_work[b] = eye
    for j in range(n):
        top = (j // 8) * 8
        sub = lax.broadcasted_iota(jnp.int32, (n - top, 1), 0) + top
        for b in range(count):
            block = work[b, top:, :]
            row = work[b, j:j + 1, :]
            pivot = row[:, j:j + 1]
            scale = lax.rsqrt(pivot)
            factor = jnp.where(sub > j, block[:, j:j + 1] * (1.0 / pivot), 0.0)
            work[b, top:, :] = jnp.where(sub == j, row * scale, block - factor * row)
            if with_inverse:
                inverse_block = inverse_work[b, top:, :]
                inverse_row = inverse_work[b, j:j + 1, :]
                inverse_work[b, top:, :] = jnp.where(
                    sub == j, inverse_row * scale, inverse_block - factor * inverse_row
                )
    for b in range(count):
        l_ref[b] = jnp.transpose(jnp.where(cols >= rows, work[b], 0.0))
        if with_inverse:
            inv_ref[b] = jnp.where(cols <= rows, inverse_work[b], 0.0)


def cholesky_batch(a, with_inverse):
    count, n, _ = a.shape
    shape = jax.ShapeDtypeStruct((count, n, n), jnp.float32)
    vmem = pl.BlockSpec(memory_space=pltpu.VMEM)
    scratch = [pltpu.VMEM((count, n, n), jnp.float32)] * (2 if with_inverse else 1)
    return pl.pallas_call(
        functools.partial(_cholesky_body, with_inverse),
        out_shape=(shape, shape) if with_inverse else shape,
        in_specs=[vmem],
        out_specs=(vmem, vmem) if with_inverse else vmem,
        scratch_shapes=scratch,
    )(a)


def per_device(panels, panel_dest, proxy_pool, proxy_index, omega, merge_maps):
    highest = lax.Precision.HIGHEST
    device_count = lax.axis_size(("leaf", "blk"))
    blk_count = lax.axis_size("blk")
    leaf_count = lax.axis_size("leaf")
    blk_index = lax.axis_index("blk")
    own_panels = panels.shape[1]
    capacity = 2 * own_panels // device_count
    rank_width = omega.shape[2]
    identity = jnp.eye(rank_width, dtype=jnp.float32)
    omega_parts = [omega[0]] + [from_shift(omega[0], "blk", shift) for shift in range(1, blk_count)]
    destination = panel_dest[:, 0]
    one_hot = (destination[:, None] == jnp.arange(device_count, dtype=jnp.int32)[None, :]).astype(
        jnp.int32
    )
    running = jnp.cumsum(one_hot, axis=0)
    slot_index = jnp.sum(running * one_hot, axis=1) - 1
    position = destination * capacity + slot_index
    outgoing = jnp.zeros((4, device_count * capacity), jnp.float32).at[:, position].set(panels)
    received = lax.all_to_all(outgoing, ("leaf", "blk"), split_axis=1, concat_axis=1, tiled=True)
    chunk = omega.shape[1]
    leaf_proxies = jnp.concatenate(
        [
            lax.dynamic_slice_in_dim(proxy_index[0], ((blk_index - shift) % blk_count) * chunk, chunk)
            for shift in range(blk_count)
        ]
    )
    points = jnp.take(proxy_pool, leaf_proxies, axis=1)
    tile = kernel_tile(received, points)
    sketch = jnp.dot(tile, jnp.concatenate(omega_parts, axis=0), preferred_element_type=jnp.float32)
    leaf_index = lax.axis_index("leaf")
    levels = leaf_count.bit_length() - 1
    path = []
    for level_index in range(levels):
        heap_index = (leaf_count >> level_index) + (leaf_index >> level_index)
        node_map = lax.dynamic_index_in_dim(merge_maps, heap_index - 2, 0, keepdims=False)
        path.append(node_map if not path else jnp.dot(path[-1], node_map, precision=highest))
    path = jnp.stack(path, axis=0)
    gram_part = jnp.dot(sketch.T, sketch, precision=highest)
    gram_sum = gram_part + from_partner(gram_part, "blk", 0)
    gram_sum = gram_sum + from_partner(gram_sum, "blk", 1)
    gram_full = gram_sum / (own_panels * blk_count) + identity
    mapped = jnp.einsum("ij,kjm->kim", gram_full, path, precision=highest)
    terms = jnp.einsum("kji,kjm->kim", path, mapped, precision=highest)
    for level_index in range(levels):
        upper = terms[level_index:]
        upper = upper + from_partner(upper, "leaf", level_index)
        terms = jnp.concatenate([terms[:level_index], upper], axis=0) if level_index else upper
    scales = jnp.asarray([0.5 ** (level_index + 1) for level_index in range(levels)], jnp.float32)
    ancestor_grams = terms * scales[:, None, None]
    lower_factor, lower_inverse = cholesky_batch(gram_full[None], True)
    basis_rows = jnp.dot(sketch, lower_inverse[0].T, precision=highest)
    returned = lax.all_to_all(
        basis_rows.astype(jnp.bfloat16), ("leaf", "blk"), split_axis=0, concat_axis=0, tiled=True
    )
    leaf_basis = jnp.take(returned, position, axis=0).astype(jnp.float32).T
    ancestor_factor = cholesky_batch(ancestor_grams, False)
    return (leaf_basis, lower_factor, ancestor_factor[None])


def solution(mesh):
    placed = (
        P(None, ("leaf", "blk")),
        P(("leaf", "blk"), None),
        P(),
        P("leaf", None),
        P("leaf", "blk", None),
        P(),
    )
    return jax.shard_map(
        per_device,
        mesh=mesh,
        in_specs=placed,
        out_specs=(P(None, ("leaf", "blk")), P("leaf", None, None), P("leaf", None, None, None)),
        check_vma=False,
    )
```

```python
import functools

import jax
import jax.numpy as jnp
from jax import lax
from jax.experimental import pallas as pl
from jax.experimental.pallas import tpu as pltpu
from jax.sharding import PartitionSpec as P


def from_partner(value, axis, bit):
    mask = 2**bit
    pairs = [(source, source ^ mask) for source in range(lax.axis_size(axis))]
    return lax.ppermute(value, axis, pairs)


def from_shift(value, axis, shift):
    size = lax.axis_size(axis)
    pairs = [(source, (source + shift) % size) for source in range(size)]
    return lax.ppermute(value, axis, pairs)


def kernel_tile(row_data, points):
    delta_x = row_data[0][:, None] - points[0][None, :]
    delta_y = row_data[1][:, None] - points[1][None, :]
    delta_z = row_data[2][:, None] - points[2][None, :]
    distance = delta_x * delta_x + delta_y * delta_y + delta_z * delta_z
    return (row_data[3][:, None] * lax.rsqrt(distance + 0.0009)).astype(jnp.bfloat16)


def _cholesky_body(with_inverse, a_ref, l_ref, *rest):
    if with_inverse:
        inv_ref, work, inverse_work = rest
    else:
        (work,) = rest
    count, n, _ = a_ref.shape
    rows = lax.broadcasted_iota(jnp.int32, (n, n), 0)
    cols = lax.broadcasted_iota(jnp.int32, (n, n), 1)
    work[...] = a_ref[...]
    if with_inverse:
        eye = jnp.where(rows == cols, 1.0, 0.0).astype(jnp.float32)
        for b in range(count):
            inverse_work[b] = eye
    for j in range(n):
        top = (j // 8) * 8
        sub = lax.broadcasted_iota(jnp.int32, (n - top, 1), 0) + top
        for b in range(count):
            block = work[b, top:, :]
            row = work[b, j:j + 1, :]
            pivot = row[:, j:j + 1]
            scale = lax.rsqrt(pivot)
            factor = jnp.where(sub > j, block[:, j:j + 1] * (1.0 / pivot), 0.0)
            work[b, top:, :] = jnp.where(sub == j, row * scale, block - factor * row)
            if with_inverse:
                inverse_block = inverse_work[b, top:, :]
                inverse_row = inverse_work[b, j:j + 1, :]
                inverse_work[b, top:, :] = jnp.where(
                    sub == j, inverse_row * scale, inverse_block - factor * inverse_row
                )
    for b in range(count):
        l_ref[b] = jnp.transpose(jnp.where(cols >= rows, work[b], 0.0))
        if with_inverse:
            inv_ref[b] = jnp.where(cols <= rows, inverse_work[b], 0.0)


def cholesky_batch(a, with_inverse):
    count, n, _ = a.shape
    shape = jax.ShapeDtypeStruct((count, n, n), jnp.float32)
    vmem = pl.BlockSpec(memory_space=pltpu.VMEM)
    scratch = [pltpu.VMEM((count, n, n), jnp.float32)] * (2 if with_inverse else 1)
    return pl.pallas_call(
        functools.partial(_cholesky_body, with_inverse),
        out_shape=(shape, shape) if with_inverse else shape,
        in_specs=[vmem],
        out_specs=(vmem, vmem) if with_inverse else vmem,
        scratch_shapes=scratch,
    )(a)


def per_device(panels, panel_dest, proxy_pool, proxy_index, omega, merge_maps):
    highest = lax.Precision.HIGHEST
    device_count = lax.axis_size(("leaf", "blk"))
    blk_count = lax.axis_size("blk")
    leaf_count = lax.axis_size("leaf")
    blk_index = lax.axis_index("blk")
    own_panels = panels.shape[1]
    capacity = 2 * own_panels // device_count
    rank_width = omega.shape[2]
    identity = jnp.eye(rank_width, dtype=jnp.float32)
    destination = panel_dest[:, 0]
    one_hot = (destination[:, None] == jnp.arange(device_count, dtype=jnp.int32)[None, :]).astype(
        jnp.int32
    )
    running = jnp.cumsum(one_hot, axis=0)
    slot_index = jnp.sum(running * one_hot, axis=1) - 1
    position = destination * capacity + slot_index
    outgoing = jnp.zeros((4, device_count * capacity), jnp.float32).at[:, position].set(panels)
    received = lax.all_to_all(outgoing, ("leaf", "blk"), split_axis=1, concat_axis=1, tiled=True)
    chunk = omega.shape[1]
    own_proxies = lax.dynamic_slice_in_dim(proxy_index[0], blk_index * chunk, chunk)
    own_points = jnp.take(proxy_pool, own_proxies, axis=1)
    omega_parts = [omega[0]] + [from_shift(omega[0], "blk", shift) for shift in range(1, blk_count)]
    point_parts = [own_points] + [from_shift(own_points, "blk", shift) for shift in range(1, blk_count)]
    points = jnp.concatenate(point_parts, axis=1)
    tile = kernel_tile(received, points)
    sketch = jnp.dot(tile, jnp.concatenate(omega_parts, axis=0), preferred_element_type=jnp.float32)
    leaf_index = lax.axis_index("leaf")
    levels = leaf_count.bit_length() - 1
    path = []
    for level_index in range(levels):
        heap_index = (leaf_count >> level_index) + (leaf_index >> level_index)
        node_map = lax.dynamic_index_in_dim(merge_maps, heap_index - 2, 0, keepdims=False)
        path.append(node_map if not path else jnp.dot(path[-1], node_map, precision=highest))
    path = jnp.stack(path, axis=0)
    gram_part = jnp.dot(sketch.T, sketch, precision=highest)
    gram_sum = gram_part + from_partner(gram_part, "blk", 0)
    gram_sum = gram_sum + from_partner(gram_sum, "blk", 1)
    gram_full = gram_sum / (own_panels * blk_count) + identity
    mapped = jnp.einsum("ij,kjm->kim", gram_full, path, precision=highest)
    terms = jnp.einsum("kji,kjm->kim", path, mapped, precision=highest)
    for level_index in range(levels):
        upper = terms[level_index:]
        upper = upper + from_partner(upper, "leaf", level_index)
        terms = jnp.concatenate([terms[:level_index], upper], axis=0) if level_index else upper
    scales = jnp.asarray([0.5 ** (level_index + 1) for level_index in range(levels)], jnp.float32)
    ancestor_grams = terms * scales[:, None, None]
    lower_factor, lower_inverse = cholesky_batch(gram_full[None], True)
    basis_rows = jnp.dot(sketch, lower_inverse[0].T, precision=highest)
    basis_rows, ancestor_grams = lax.optimization_barrier((basis_rows, ancestor_grams))
    returned = lax.all_to_all(
        basis_rows.astype(jnp.bfloat16), ("leaf", "blk"), split_axis=0, concat_axis=0, tiled=True
    )
    leaf_basis = jnp.take(returned.astype(jnp.float32), position, axis=0).T
    ancestor_factor = cholesky_batch(ancestor_grams, False)
    return (leaf_basis, lower_factor, ancestor_factor[None])


def solution(mesh):
    placed = (
        P(None, ("leaf", "blk")),
        P(("leaf", "blk"), None),
        P(),
        P("leaf", None),
        P("leaf", "blk", None),
        P(),
    )
    return jax.shard_map(
        per_device,
        mesh=mesh,
        in_specs=placed,
        out_specs=(P(None, ("leaf", "blk")), P("leaf", None, None), P("leaf", None, None, None)),
        check_vma=False,
    )
```

```python
import functools

import jax
import jax.numpy as jnp
from jax import lax
from jax.experimental import pallas as pl
from jax.experimental.pallas import tpu as pltpu
from jax.sharding import PartitionSpec as P


def from_partner(value, axis, bit):
    mask = 2**bit
    pairs = [(source, source ^ mask) for source in range(lax.axis_size(axis))]
    return lax.ppermute(value, axis, pairs)


def from_shift(value, axis, shift):
    size = lax.axis_size(axis)
    pairs = [(source, (source + shift) % size) for source in range(size)]
    return lax.ppermute(value, axis, pairs)


def kernel_tile(row_data, points):
    delta_x = row_data[0][:, None] - points[0][None, :]
    delta_y = row_data[1][:, None] - points[1][None, :]
    delta_z = row_data[2][:, None] - points[2][None, :]
    distance = delta_x * delta_x + delta_y * delta_y + delta_z * delta_z
    return (row_data[3][:, None] * lax.rsqrt(distance + 0.0009)).astype(jnp.bfloat16)


def _cholesky_body(with_inverse, a_ref, l_ref, *rest):
    if with_inverse:
        inv_ref, work, inverse_work = rest
    else:
        (work,) = rest
    count, n, _ = a_ref.shape
    rows = lax.broadcasted_iota(jnp.int32, (n, n), 0)
    cols = lax.broadcasted_iota(jnp.int32, (n, n), 1)
    work[...] = a_ref[...]
    if with_inverse:
        eye = jnp.where(rows == cols, 1.0, 0.0).astype(jnp.float32)
        for b in range(count):
            inverse_work[b] = eye
    for j in range(n):
        top = (j // 8) * 8
        sub = lax.broadcasted_iota(jnp.int32, (n - top, 1), 0) + top
        for b in range(count):
            block = work[b, top:, :]
            row = work[b, j:j + 1, :]
            pivot = row[:, j:j + 1]
            scale = lax.rsqrt(pivot)
            factor = jnp.where(sub > j, block[:, j:j + 1] * (1.0 / pivot), 0.0)
            work[b, top:, :] = jnp.where(sub == j, row * scale, block - factor * row)
            if with_inverse:
                inverse_block = inverse_work[b, top:, :]
                inverse_row = inverse_work[b, j:j + 1, :]
                inverse_work[b, top:, :] = jnp.where(
                    sub == j, inverse_row * scale, inverse_block - factor * inverse_row
                )
    for b in range(count):
        l_ref[b] = jnp.transpose(jnp.where(cols >= rows, work[b], 0.0))
        if with_inverse:
            inv_ref[b] = jnp.where(cols <= rows, inverse_work[b], 0.0)


def cholesky_batch(a, with_inverse):
    count, n, _ = a.shape
    shape = jax.ShapeDtypeStruct((count, n, n), jnp.float32)
    vmem = pl.BlockSpec(memory_space=pltpu.VMEM)
    scratch = [pltpu.VMEM((count, n, n), jnp.float32)] * (2 if with_inverse else 1)
    return pl.pallas_call(
        functools.partial(_cholesky_body, with_inverse),
        out_shape=(shape, shape) if with_inverse else shape,
        in_specs=[vmem],
        out_specs=(vmem, vmem) if with_inverse else vmem,
        scratch_shapes=scratch,
    )(a)


def _leaf_chunk_body(first, last, a_ref, x_ref, a_out, x_out):
    n = a_ref.shape[1]
    rows = lax.broadcasted_iota(jnp.int32, (n, n), 0)
    cols = lax.broadcasted_iota(jnp.int32, (n, n), 1)
    a_out[...] = a_ref[...]
    if first == 0:
        x_out[0] = jnp.where(rows == cols, 1.0, 0.0).astype(jnp.float32)
    else:
        x_out[...] = x_ref[...]
    for j in range(first, last):
        top = (j // 8) * 8
        sub = lax.broadcasted_iota(jnp.int32, (n - top, 1), 0) + top
        block = a_out[0, top:, :]
        row = a_out[0, j:j + 1, :]
        pivot = row[:, j:j + 1]
        scale = lax.rsqrt(pivot)
        factor = jnp.where(sub > j, block[:, j:j + 1] * (1.0 / pivot), 0.0)
        a_out[0, top:, :] = jnp.where(sub == j, row * scale, block - factor * row)
        inverse_block = x_out[0, top:, :]
        inverse_row = x_out[0, j:j + 1, :]
        x_out[0, top:, :] = jnp.where(
            sub == j, inverse_row * scale, inverse_block - factor * inverse_row
        )
    if last == n:
        a_out[0] = jnp.transpose(jnp.where(cols >= rows, a_out[0], 0.0))
        x_out[0] = jnp.where(cols <= rows, x_out[0], 0.0)


def leaf_chunk(work, inverse_work, first, last):
    shape = jax.ShapeDtypeStruct(work.shape, jnp.float32)
    vmem = pl.BlockSpec(memory_space=pltpu.VMEM)
    return pl.pallas_call(
        functools.partial(_leaf_chunk_body, first, last),
        out_shape=(shape, shape),
        in_specs=[vmem, vmem],
        out_specs=(vmem, vmem),
    )(work, inverse_work)


def chunk_bounds(n, parts):
    cost = [n // 8 - j // 8 + 4 for j in range(n)]
    total, bounds, running = sum(cost), [0], 0
    for j in range(n):
        running += cost[j]
        if running >= total * len(bounds) / parts and len(bounds) < parts:
            bounds.append(j + 1)
    return bounds + [n]


def per_device(panels, panel_dest, proxy_pool, proxy_index, omega, merge_maps):
    highest = lax.Precision.HIGHEST
    device_count = lax.axis_size(("leaf", "blk"))
    blk_count = lax.axis_size("blk")
    leaf_count = lax.axis_size("leaf")
    blk_index = lax.axis_index("blk")
    own_panels = panels.shape[1]
    capacity = 2 * own_panels // device_count
    rank_width = omega.shape[2]
    identity = jnp.eye(rank_width, dtype=jnp.float32)
    destination = panel_dest[:, 0]
    one_hot = (destination[:, None] == jnp.arange(device_count, dtype=jnp.int32)[None, :]).astype(
        jnp.int32
    )
    running = jnp.cumsum(one_hot, axis=0)
    slot_index = jnp.sum(running * one_hot, axis=1) - 1
    position = destination * capacity + slot_index
    outgoing = jnp.zeros((4, device_count * capacity), jnp.float32).at[:, position].set(panels)
    received = lax.all_to_all(outgoing, ("leaf", "blk"), split_axis=1, concat_axis=1, tiled=True)
    chunk = omega.shape[1]
    own_proxies = lax.dynamic_slice_in_dim(proxy_index[0], blk_index * chunk, chunk)
    own_points = jnp.take(proxy_pool, own_proxies, axis=1)
    omega_parts = [omega[0]] + [from_shift(omega[0], "blk", shift) for shift in range(1, blk_count)]
    point_parts = [own_points] + [from_shift(own_points, "blk", shift) for shift in range(1, blk_count)]
    points = jnp.concatenate(point_parts, axis=1)
    tile = kernel_tile(received, points)
    sketch = jnp.dot(tile, jnp.concatenate(omega_parts, axis=0), preferred_element_type=jnp.float32)
    leaf_index = lax.axis_index("leaf")
    levels = leaf_count.bit_length() - 1
    path = []
    for level_index in range(levels):
        heap_index = (leaf_count >> level_index) + (leaf_index >> level_index)
        node_map = lax.dynamic_index_in_dim(merge_maps, heap_index - 2, 0, keepdims=False)
        path.append(node_map if not path else jnp.dot(path[-1], node_map, precision=highest))
    path = jnp.stack(path, axis=0)
    gram_part = jnp.dot(sketch.T, sketch, precision=highest)
    gram_sum = gram_part + from_partner(gram_part, "blk", 0)
    gram_sum = gram_sum + from_partner(gram_sum, "blk", 1)
    gram_full = gram_sum / (own_panels * blk_count) + identity
    mapped = jnp.einsum("ij,kjm->kim", gram_full, path, precision=highest)
    terms = jnp.einsum("kji,kjm->kim", path, mapped, precision=highest)
    bounds = chunk_bounds(rank_width, levels)
    work, inverse_work = gram_full[None], gram_full[None]
    for level_index in range(levels):
        upper = terms[level_index:]
        received_terms = from_partner(upper, "leaf", level_index)
        work, inverse_work = leaf_chunk(
            work, inverse_work, bounds[level_index], bounds[level_index + 1]
        )
        work, inverse_work, received_terms = lax.optimization_barrier(
            (work, inverse_work, received_terms)
        )
        upper = upper + received_terms
        terms = jnp.concatenate([terms[:level_index], upper], axis=0) if level_index else upper
    scales = jnp.asarray([0.5 ** (level_index + 1) for level_index in range(levels)], jnp.float32)
    ancestor_grams = terms * scales[:, None, None]
    lower_factor, lower_inverse = work, inverse_work
    basis_rows = jnp.dot(sketch, lower_inverse[0].T, precision=highest)
    basis_rows, ancestor_grams = lax.optimization_barrier((basis_rows, ancestor_grams))
    returned = lax.all_to_all(
        basis_rows.astype(jnp.bfloat16), ("leaf", "blk"), split_axis=0, concat_axis=0, tiled=True
    )
    leaf_basis = jnp.take(returned.astype(jnp.float32), position, axis=0).T
    ancestor_factor = cholesky_batch(ancestor_grams, False)
    return (leaf_basis, lower_factor, ancestor_factor[None])


def solution(mesh):
    placed = (
        P(None, ("leaf", "blk")),
        P(("leaf", "blk"), None),
        P(),
        P("leaf", None),
        P("leaf", "blk", None),
        P(),
    )
    return jax.shard_map(
        per_device,
        mesh=mesh,
        in_specs=placed,
        out_specs=(P(None, ("leaf", "blk")), P("leaf", None, None), P("leaf", None, None, None)),
        check_vma=False,
    )
```

```python
import functools

import jax
import jax.numpy as jnp
from jax import lax
from jax.experimental import pallas as pl
from jax.experimental.pallas import tpu as pltpu
from jax.sharding import PartitionSpec as P


def from_partner(value, axis, bit):
    mask = 2**bit
    pairs = [(source, source ^ mask) for source in range(lax.axis_size(axis))]
    return lax.ppermute(value, axis, pairs)


def group_sums(value, axis, bits):
    low = value + from_partner(value, axis, bits[0])
    if len(bits) == 1:
        return low, low
    high = from_partner(value, axis, bits[1]) + lax.ppermute(
        value,
        axis,
        [(source, source ^ (2 ** bits[0] + 2 ** bits[1])) for source in range(lax.axis_size(axis))],
    )
    return low, low + high


def from_shift(value, axis, shift):
    size = lax.axis_size(axis)
    pairs = [(source, (source + shift) % size) for source in range(size)]
    return lax.ppermute(value, axis, pairs)


def kernel_tile(row_data, points):
    delta_x = row_data[0][:, None] - points[0][None, :]
    delta_y = row_data[1][:, None] - points[1][None, :]
    delta_z = row_data[2][:, None] - points[2][None, :]
    distance = delta_x * delta_x + delta_y * delta_y + delta_z * delta_z
    return (row_data[3][:, None] * lax.rsqrt(distance + 0.0009)).astype(jnp.bfloat16)


def _cholesky_body(with_inverse, a_ref, l_ref, *rest):
    if with_inverse:
        inv_ref, work, inverse_work = rest
    else:
        (work,) = rest
    count, n, _ = a_ref.shape
    rows = lax.broadcasted_iota(jnp.int32, (n, n), 0)
    cols = lax.broadcasted_iota(jnp.int32, (n, n), 1)
    work[...] = a_ref[...]
    if with_inverse:
        eye = jnp.where(rows == cols, 1.0, 0.0).astype(jnp.float32)
        for b in range(count):
            inverse_work[b] = eye
    for j in range(n):
        top = (j // 8) * 8
        sub = lax.broadcasted_iota(jnp.int32, (n - top, 1), 0) + top
        for b in range(count):
            block = work[b, top:, :]
            row = work[b, j:j + 1, :]
            pivot = row[:, j:j + 1]
            scale = lax.rsqrt(pivot)
            factor = jnp.where(sub > j, block[:, j:j + 1] * (1.0 / pivot), 0.0)
            work[b, top:, :] = jnp.where(sub == j, row * scale, block - factor * row)
            if with_inverse:
                inverse_block = inverse_work[b, top:, :]
                inverse_row = inverse_work[b, j:j + 1, :]
                inverse_work[b, top:, :] = jnp.where(
                    sub == j, inverse_row * scale, inverse_block - factor * inverse_row
                )
    for b in range(count):
        l_ref[b] = jnp.transpose(jnp.where(cols >= rows, work[b], 0.0))
        if with_inverse:
            inv_ref[b] = jnp.where(cols <= rows, inverse_work[b], 0.0)


def cholesky_batch(a, with_inverse):
    count, n, _ = a.shape
    shape = jax.ShapeDtypeStruct((count, n, n), jnp.float32)
    vmem = pl.BlockSpec(memory_space=pltpu.VMEM)
    scratch = [pltpu.VMEM((count, n, n), jnp.float32)] * (2 if with_inverse else 1)
    return pl.pallas_call(
        functools.partial(_cholesky_body, with_inverse),
        out_shape=(shape, shape) if with_inverse else shape,
        in_specs=[vmem],
        out_specs=(vmem, vmem) if with_inverse else vmem,
        scratch_shapes=scratch,
    )(a)


def _leaf_chunk_body(first, last, a_ref, x_ref, a_out, x_out):
    n = a_ref.shape[1]
    rows = lax.broadcasted_iota(jnp.int32, (n, n), 0)
    cols = lax.broadcasted_iota(jnp.int32, (n, n), 1)
    a_out[...] = a_ref[...]
    if first == 0:
        x_out[0] = jnp.where(rows == cols, 1.0, 0.0).astype(jnp.float32)
    else:
        x_out[...] = x_ref[...]
    for j in range(first, last):
        top = (j // 8) * 8
        sub = lax.broadcasted_iota(jnp.int32, (n - top, 1), 0) + top
        block = a_out[0, top:, :]
        row = a_out[0, j:j + 1, :]
        pivot = row[:, j:j + 1]
        scale = lax.rsqrt(pivot)
        factor = jnp.where(sub > j, block[:, j:j + 1] * (1.0 / pivot), 0.0)
        a_out[0, top:, :] = jnp.where(sub == j, row * scale, block - factor * row)
        inverse_block = x_out[0, top:, :]
        inverse_row = x_out[0, j:j + 1, :]
        x_out[0, top:, :] = jnp.where(
            sub == j, inverse_row * scale, inverse_block - factor * inverse_row
        )
    if last == n:
        a_out[0] = jnp.transpose(jnp.where(cols >= rows, a_out[0], 0.0))
        x_out[0] = jnp.where(cols <= rows, x_out[0], 0.0)


def leaf_chunk(work, inverse_work, first, last):
    shape = jax.ShapeDtypeStruct(work.shape, jnp.float32)
    vmem = pl.BlockSpec(memory_space=pltpu.VMEM)
    return pl.pallas_call(
        functools.partial(_leaf_chunk_body, first, last),
        out_shape=(shape, shape),
        in_specs=[vmem, vmem],
        out_specs=(vmem, vmem),
    )(work, inverse_work)


def chunk_bounds(n, parts):
    cost = [n // 8 - j // 8 + 4 for j in range(n)]
    total, bounds, running = sum(cost), [0], 0
    for j in range(n):
        running += cost[j]
        if running >= total * len(bounds) / parts and len(bounds) < parts:
            bounds.append(j + 1)
    return bounds + [n]


def per_device(panels, panel_dest, proxy_pool, proxy_index, omega, merge_maps):
    highest = lax.Precision.HIGHEST
    device_count = lax.axis_size(("leaf", "blk"))
    blk_count = lax.axis_size("blk")
    leaf_count = lax.axis_size("leaf")
    blk_index = lax.axis_index("blk")
    own_panels = panels.shape[1]
    capacity = 2 * own_panels // device_count
    rank_width = omega.shape[2]
    identity = jnp.eye(rank_width, dtype=jnp.float32)
    destination = panel_dest[:, 0]
    one_hot = (destination[:, None] == jnp.arange(device_count, dtype=jnp.int32)[None, :]).astype(
        jnp.int32
    )
    running = jnp.cumsum(one_hot, axis=0)
    slot_index = jnp.sum(running * one_hot, axis=1) - 1
    position = destination * capacity + slot_index
    outgoing = jnp.zeros((4, device_count * capacity), jnp.float32).at[:, position].set(panels)
    received = lax.all_to_all(outgoing, ("leaf", "blk"), split_axis=1, concat_axis=1, tiled=True)
    chunk = omega.shape[1]
    own_proxies = lax.dynamic_slice_in_dim(proxy_index[0], blk_index * chunk, chunk)
    own_points = jnp.take(proxy_pool, own_proxies, axis=1)
    omega_parts = [omega[0]] + [from_shift(omega[0], "blk", shift) for shift in range(1, blk_count)]
    point_parts = [own_points] + [from_shift(own_points, "blk", shift) for shift in range(1, blk_count)]
    points = jnp.concatenate(point_parts, axis=1)
    tile = kernel_tile(received, points)
    sketch = jnp.dot(tile, jnp.concatenate(omega_parts, axis=0), preferred_element_type=jnp.float32)
    leaf_index = lax.axis_index("leaf")
    levels = leaf_count.bit_length() - 1
    path = []
    for level_index in range(levels):
        heap_index = (leaf_count >> level_index) + (leaf_index >> level_index)
        node_map = lax.dynamic_index_in_dim(merge_maps, heap_index - 2, 0, keepdims=False)
        path.append(node_map if not path else jnp.dot(path[-1], node_map, precision=highest))
    path = jnp.stack(path, axis=0)
    gram_part = jnp.dot(sketch.T, sketch, precision=highest)
    _, gram_sum = group_sums(gram_part, "blk", (0, 1))
    gram_full = gram_sum / (own_panels * blk_count) + identity
    mapped = jnp.einsum("ij,kjm->kim", gram_full, path, precision=highest)
    terms = jnp.einsum("kji,kjm->kim", path, mapped, precision=highest)
    stages = [(0, 1), (2, 3), (4,)]
    bounds = chunk_bounds(rank_width, len(stages))
    work, inverse_work = gram_full[None], gram_full[None]
    finished = []
    for stage_index, bits in enumerate(stages):
        pending = terms
        work, inverse_work = leaf_chunk(
            work, inverse_work, bounds[stage_index], bounds[stage_index + 1]
        )
        low, full = group_sums(pending, "leaf", bits)
        work, inverse_work, low, full = lax.optimization_barrier((work, inverse_work, low, full))
        finished.append(low[:1])
        if len(bits) == 2:
            finished.append(full[1:2])
        terms = full[len(bits):]
    terms = jnp.concatenate(finished, axis=0)
    scales = jnp.asarray([0.5 ** (level_index + 1) for level_index in range(levels)], jnp.float32)
    ancestor_grams = terms * scales[:, None, None]
    lower_factor, lower_inverse = work, inverse_work
    basis_rows = jnp.dot(sketch, lower_inverse[0].T, precision=highest)
    basis_rows, ancestor_grams = lax.optimization_barrier((basis_rows, ancestor_grams))
    returned = lax.all_to_all(
        basis_rows.astype(jnp.bfloat16), ("leaf", "blk"), split_axis=0, concat_axis=0, tiled=True
    )
    leaf_basis = jnp.take(returned.astype(jnp.float32), position, axis=0).T
    ancestor_factor = cholesky_batch(ancestor_grams, False)
    return (leaf_basis, lower_factor, ancestor_factor[None])


def solution(mesh):
    placed = (
        P(None, ("leaf", "blk")),
        P(("leaf", "blk"), None),
        P(),
        P("leaf", None),
        P("leaf", "blk", None),
        P(),
    )
    return jax.shard_map(
        per_device,
        mesh=mesh,
        in_specs=placed,
        out_specs=(P(None, ("leaf", "blk")), P("leaf", None, None), P("leaf", None, None, None)),
        check_vma=False,
    )
```

```python
import functools

import jax
import jax.numpy as jnp
from jax import lax
from jax.experimental import pallas as pl
from jax.experimental.pallas import tpu as pltpu
from jax.sharding import PartitionSpec as P


def from_partner(value, axis, bit):
    mask = 2**bit
    pairs = [(source, source ^ mask) for source in range(lax.axis_size(axis))]
    return lax.ppermute(value, axis, pairs)


def from_shift(value, axis, shift):
    size = lax.axis_size(axis)
    pairs = [(source, (source + shift) % size) for source in range(size)]
    return lax.ppermute(value, axis, pairs)


def kernel_tile(row_data, points):
    delta_x = row_data[0][:, None] - points[0][None, :]
    delta_y = row_data[1][:, None] - points[1][None, :]
    delta_z = row_data[2][:, None] - points[2][None, :]
    distance = delta_x * delta_x + delta_y * delta_y + delta_z * delta_z
    return (row_data[3][:, None] * lax.rsqrt(distance + 0.0009)).astype(jnp.bfloat16)


def _cholesky_body(with_inverse, a_ref, l_ref, *rest):
    if with_inverse:
        inv_ref, work, inverse_work = rest
    else:
        (work,) = rest
    count, n, _ = a_ref.shape
    rows = lax.broadcasted_iota(jnp.int32, (n, n), 0)
    cols = lax.broadcasted_iota(jnp.int32, (n, n), 1)
    work[...] = a_ref[...]
    if with_inverse:
        eye = jnp.where(rows == cols, 1.0, 0.0).astype(jnp.float32)
        for b in range(count):
            inverse_work[b] = eye
    for j in range(n):
        top = (j // 8) * 8
        sub = lax.broadcasted_iota(jnp.int32, (n - top, 1), 0) + top
        for b in range(count):
            block = work[b, top:, :]
            row = work[b, j:j + 1, :]
            pivot = row[:, j:j + 1]
            scale = lax.rsqrt(pivot)
            factor = jnp.where(sub > j, block[:, j:j + 1] * (1.0 / pivot), 0.0)
            work[b, top:, :] = jnp.where(sub == j, row * scale, block - factor * row)
            if with_inverse:
                inverse_block = inverse_work[b, top:, :]
                inverse_row = inverse_work[b, j:j + 1, :]
                inverse_work[b, top:, :] = jnp.where(
                    sub == j, inverse_row * scale, inverse_block - factor * inverse_row
                )
    for b in range(count):
        l_ref[b] = jnp.transpose(jnp.where(cols >= rows, work[b], 0.0))
        if with_inverse:
            inv_ref[b] = jnp.where(cols <= rows, inverse_work[b], 0.0)


def cholesky_batch(a, with_inverse):
    count, n, _ = a.shape
    shape = jax.ShapeDtypeStruct((count, n, n), jnp.float32)
    vmem = pl.BlockSpec(memory_space=pltpu.VMEM)
    scratch = [pltpu.VMEM((count, n, n), jnp.float32)] * (2 if with_inverse else 1)
    return pl.pallas_call(
        functools.partial(_cholesky_body, with_inverse),
        out_shape=(shape, shape) if with_inverse else shape,
        in_specs=[vmem],
        out_specs=(vmem, vmem) if with_inverse else vmem,
        scratch_shapes=scratch,
    )(a)


def per_device(panels, panel_dest, proxy_pool, proxy_index, omega, merge_maps):
    highest = lax.Precision.HIGHEST
    device_count = lax.axis_size(("leaf", "blk"))
    blk_count = lax.axis_size("blk")
    leaf_count = lax.axis_size("leaf")
    blk_index = lax.axis_index("blk")
    own_panels = panels.shape[1]
    capacity = 2 * own_panels // device_count
    rank_width = omega.shape[2]
    identity = jnp.eye(rank_width, dtype=jnp.float32)
    omega_parts = [omega[0]] + [from_shift(omega[0], "blk", shift) for shift in range(1, blk_count)]
    destination = panel_dest[:, 0] // blk_count
    capacity = blk_count * capacity
    one_hot = (destination[:, None] == jnp.arange(leaf_count, dtype=jnp.int32)[None, :]).astype(
        jnp.int32
    )
    running = jnp.cumsum(one_hot, axis=0)
    slot_index = jnp.sum(running * one_hot, axis=1) - 1
    position = destination * capacity + slot_index
    outgoing = jnp.zeros((4, leaf_count * capacity), jnp.float32).at[:, position].set(panels)
    received = lax.all_to_all(outgoing, "leaf", split_axis=1, concat_axis=1, tiled=True)
    chunk = omega.shape[1]
    leaf_proxies = jnp.concatenate(
        [
            lax.dynamic_slice_in_dim(proxy_index[0], ((blk_index - shift) % blk_count) * chunk, chunk)
            for shift in range(blk_count)
        ]
    )
    points = jnp.take(proxy_pool, leaf_proxies, axis=1)
    tile = kernel_tile(received, points)
    sketch = jnp.dot(tile, jnp.concatenate(omega_parts, axis=0), preferred_element_type=jnp.float32)
    leaf_index = lax.axis_index("leaf")
    levels = leaf_count.bit_length() - 1
    path = []
    for level_index in range(levels):
        heap_index = (leaf_count >> level_index) + (leaf_index >> level_index)
        node_map = lax.dynamic_index_in_dim(merge_maps, heap_index - 2, 0, keepdims=False)
        path.append(node_map if not path else jnp.dot(path[-1], node_map, precision=highest))
    path = jnp.stack(path, axis=0)
    gram_part = jnp.dot(sketch.T, sketch, precision=highest)
    gram_sum = gram_part + from_partner(gram_part, "blk", 0)
    gram_sum = gram_sum + from_partner(gram_sum, "blk", 1)
    gram_full = gram_sum / (own_panels * blk_count) + identity
    mapped = jnp.einsum("ij,kjm->kim", gram_full, path, precision=highest)
    terms = jnp.einsum("kji,kjm->kim", path, mapped, precision=highest)
    for level_index in range(levels):
        upper = terms[level_index:]
        upper = upper + from_partner(upper, "leaf", level_index)
        terms = jnp.concatenate([terms[:level_index], upper], axis=0) if level_index else upper
    scales = jnp.asarray([0.5 ** (level_index + 1) for level_index in range(levels)], jnp.float32)
    ancestor_grams = terms * scales[:, None, None]
    lower_factor, lower_inverse = cholesky_batch(gram_full[None], True)
    basis_rows = jnp.dot(sketch, lower_inverse[0].T, precision=highest)
    returned = lax.all_to_all(
        basis_rows.astype(jnp.bfloat16), "leaf", split_axis=0, concat_axis=0, tiled=True
    )
    leaf_basis = jnp.take(returned, position, axis=0).astype(jnp.float32).T
    ancestor_factor = cholesky_batch(ancestor_grams, False)
    return (leaf_basis, lower_factor, ancestor_factor[None])


def solution(mesh):
    placed = (
        P(None, ("leaf", "blk")),
        P(("leaf", "blk"), None),
        P(),
        P("leaf", None),
        P("leaf", "blk", None),
        P(),
    )
    return jax.shard_map(
        per_device,
        mesh=mesh,
        in_specs=placed,
        out_specs=(P(None, ("leaf", "blk")), P("leaf", None, None), P("leaf", None, None, None)),
        check_vma=False,
    )
```

```python
import functools

import jax
import jax.numpy as jnp
from jax import lax
from jax.experimental import pallas as pl
from jax.experimental.pallas import tpu as pltpu
from jax.sharding import PartitionSpec as P


def from_partner(value, axis, bit):
    mask = 2**bit
    pairs = [(source, source ^ mask) for source in range(lax.axis_size(axis))]
    return lax.ppermute(value, axis, pairs)


def from_shift(value, axis, shift):
    size = lax.axis_size(axis)
    pairs = [(source, (source + shift) % size) for source in range(size)]
    return lax.ppermute(value, axis, pairs)


def kernel_tile(row_data, points):
    delta_x = row_data[0][:, None] - points[0][None, :]
    delta_y = row_data[1][:, None] - points[1][None, :]
    delta_z = row_data[2][:, None] - points[2][None, :]
    distance = delta_x * delta_x + delta_y * delta_y + delta_z * delta_z
    return (row_data[3][:, None] * lax.rsqrt(distance + 0.0009)).astype(jnp.bfloat16)


def _cholesky_body(with_inverse, a_ref, l_ref, *rest):
    if with_inverse:
        inv_ref, work, inverse_work = rest
    else:
        (work,) = rest
    count, n, _ = a_ref.shape
    rows = lax.broadcasted_iota(jnp.int32, (n, n), 0)
    cols = lax.broadcasted_iota(jnp.int32, (n, n), 1)
    work[...] = a_ref[...]
    if with_inverse:
        eye = jnp.where(rows == cols, 1.0, 0.0).astype(jnp.float32)
        for b in range(count):
            inverse_work[b] = eye
    for j in range(n):
        top = (j // 8) * 8
        sub = lax.broadcasted_iota(jnp.int32, (n - top, 1), 0) + top
        for b in range(count):
            block = work[b, top:, :]
            row = work[b, j:j + 1, :]
            pivot = row[:, j:j + 1]
            scale = lax.rsqrt(pivot)
            factor = jnp.where(sub > j, block[:, j:j + 1] * (1.0 / pivot), 0.0)
            work[b, top:, :] = jnp.where(sub == j, row * scale, block - factor * row)
            if with_inverse:
                inverse_block = inverse_work[b, top:, :]
                inverse_row = inverse_work[b, j:j + 1, :]
                inverse_work[b, top:, :] = jnp.where(
                    sub == j, inverse_row * scale, inverse_block - factor * inverse_row
                )
    for b in range(count):
        l_ref[b] = jnp.transpose(jnp.where(cols >= rows, work[b], 0.0))
        if with_inverse:
            inv_ref[b] = jnp.where(cols <= rows, inverse_work[b], 0.0)


def cholesky_batch(a, with_inverse):
    count, n, _ = a.shape
    shape = jax.ShapeDtypeStruct((count, n, n), jnp.float32)
    vmem = pl.BlockSpec(memory_space=pltpu.VMEM)
    scratch = [pltpu.VMEM((count, n, n), jnp.float32)] * (2 if with_inverse else 1)
    return pl.pallas_call(
        functools.partial(_cholesky_body, with_inverse),
        out_shape=(shape, shape) if with_inverse else shape,
        in_specs=[vmem],
        out_specs=(vmem, vmem) if with_inverse else vmem,
        scratch_shapes=scratch,
    )(a)


def per_device(panels, panel_dest, proxy_pool, proxy_index, omega, merge_maps):
    highest = lax.Precision.HIGHEST
    device_count = lax.axis_size(("leaf", "blk"))
    blk_count = lax.axis_size("blk")
    leaf_count = lax.axis_size("leaf")
    blk_index = lax.axis_index("blk")
    own_panels = panels.shape[1]
    capacity = 2 * own_panels // device_count
    rank_width = omega.shape[2]
    identity = jnp.eye(rank_width, dtype=jnp.float32)
    destination = panel_dest[:, 0]
    one_hot = (destination[:, None] == jnp.arange(device_count, dtype=jnp.int32)[None, :]).astype(
        jnp.int32
    )
    running = jnp.cumsum(one_hot, axis=0)
    slot_index = jnp.sum(running * one_hot, axis=1) - 1
    position = destination * capacity + slot_index
    outgoing = jnp.zeros((4, device_count * capacity), jnp.float32).at[:, position].set(panels)
    received = lax.all_to_all(outgoing, ("leaf", "blk"), split_axis=1, concat_axis=1, tiled=True)
    chunk = omega.shape[1]
    own_proxies = lax.dynamic_slice_in_dim(proxy_index[0], blk_index * chunk, chunk)
    own_points = jnp.take(proxy_pool, own_proxies, axis=1)
    omega_parts = [omega[0]] + [from_shift(omega[0], "blk", shift) for shift in range(1, blk_count)]
    point_parts = [own_points] + [from_shift(own_points, "blk", shift) for shift in range(1, blk_count)]
    points = jnp.concatenate(point_parts, axis=1)
    tile = kernel_tile(received, points)
    sketch = jnp.dot(tile, jnp.concatenate(omega_parts, axis=0), preferred_element_type=jnp.float32)
    leaf_index = lax.axis_index("leaf")
    levels = leaf_count.bit_length() - 1
    path = []
    for level_index in range(levels):
        heap_index = (leaf_count >> level_index) + (leaf_index >> level_index)
        node_map = lax.dynamic_index_in_dim(merge_maps, heap_index - 2, 0, keepdims=False)
        path.append(node_map if not path else jnp.dot(path[-1], node_map, precision=highest))
    path = jnp.stack(path, axis=0)
    gram_part = jnp.dot(sketch.T, sketch, precision=highest)
    gram_sum = gram_part + from_partner(gram_part, "blk", 0)
    gram_sum = gram_sum + from_partner(gram_sum, "blk", 1)
    gram_full = gram_sum / (own_panels * blk_count) + identity
    lower_factor, lower_inverse = cholesky_batch(gram_full[None], True)
    lower_factor, lower_inverse, tree_gram = lax.optimization_barrier(
        (lower_factor, lower_inverse, gram_full)
    )
    mapped = jnp.einsum("ij,kjm->kim", tree_gram, path, precision=highest)
    terms = jnp.einsum("kji,kjm->kim", path, mapped, precision=highest)
    for level_index in range(levels):
        upper = terms[level_index:]
        upper = upper + from_partner(upper, "leaf", level_index)
        terms = jnp.concatenate([terms[:level_index], upper], axis=0) if level_index else upper
    scales = jnp.asarray([0.5 ** (level_index + 1) for level_index in range(levels)], jnp.float32)
    ancestor_grams = terms * scales[:, None, None]
    basis_rows = jnp.dot(sketch, lower_inverse[0].T, precision=highest)
    basis_rows, ancestor_grams = lax.optimization_barrier((basis_rows, ancestor_grams))
    returned = lax.all_to_all(
        basis_rows.astype(jnp.bfloat16), ("leaf", "blk"), split_axis=0, concat_axis=0, tiled=True
    )
    leaf_basis = jnp.take(returned.astype(jnp.float32), position, axis=0).T
    ancestor_factor = cholesky_batch(ancestor_grams, False)
    return (leaf_basis, lower_factor, ancestor_factor[None])


def solution(mesh):
    placed = (
        P(None, ("leaf", "blk")),
        P(("leaf", "blk"), None),
        P(),
        P("leaf", None),
        P("leaf", "blk", None),
        P(),
    )
    return jax.shard_map(
        per_device,
        mesh=mesh,
        in_specs=placed,
        out_specs=(P(None, ("leaf", "blk")), P("leaf", None, None), P("leaf", None, None, None)),
        check_vma=False,
    )
```

```python
import functools

import jax
import jax.numpy as jnp
from jax import lax
from jax.experimental import pallas as pl
from jax.experimental.pallas import tpu as pltpu
from jax.sharding import PartitionSpec as P


def from_partner(value, axis, bit):
    mask = 2**bit
    pairs = [(source, source ^ mask) for source in range(lax.axis_size(axis))]
    return lax.ppermute(value, axis, pairs)


def from_shift(value, axis, shift):
    size = lax.axis_size(axis)
    pairs = [(source, (source + shift) % size) for source in range(size)]
    return lax.ppermute(value, axis, pairs)


def kernel_tile(row_data, points):
    delta_x = row_data[0][:, None] - points[0][None, :]
    delta_y = row_data[1][:, None] - points[1][None, :]
    delta_z = row_data[2][:, None] - points[2][None, :]
    distance = delta_x * delta_x + delta_y * delta_y + delta_z * delta_z
    return (row_data[3][:, None] * lax.rsqrt(distance + 0.0009)).astype(jnp.bfloat16)


def _cholesky_body(with_inverse, a_ref, l_ref, *rest):
    if with_inverse:
        inv_ref, work, inverse_work = rest
    else:
        (work,) = rest
    count, n, _ = a_ref.shape
    rows = lax.broadcasted_iota(jnp.int32, (n, n), 0)
    cols = lax.broadcasted_iota(jnp.int32, (n, n), 1)
    work[...] = a_ref[...]
    if with_inverse:
        eye = jnp.where(rows == cols, 1.0, 0.0).astype(jnp.float32)
        for b in range(count):
            inverse_work[b] = eye
    for j in range(n):
        top = (j // 8) * 8
        sub = lax.broadcasted_iota(jnp.int32, (n - top, 1), 0) + top
        for b in range(count):
            block = work[b, top:, :]
            row = work[b, j:j + 1, :]
            pivot = row[:, j:j + 1]
            scale = lax.rsqrt(pivot)
            factor = jnp.where(sub > j, block[:, j:j + 1] * (1.0 / pivot), 0.0)
            work[b, top:, :] = jnp.where(sub == j, row * scale, block - factor * row)
            if with_inverse:
                inverse_block = inverse_work[b, top:, :]
                inverse_row = inverse_work[b, j:j + 1, :]
                inverse_work[b, top:, :] = jnp.where(
                    sub == j, inverse_row * scale, inverse_block - factor * inverse_row
                )
    for b in range(count):
        l_ref[b] = jnp.transpose(jnp.where(cols >= rows, work[b], 0.0))
        if with_inverse:
            inv_ref[b] = jnp.where(cols <= rows, inverse_work[b], 0.0)


def cholesky_batch(a, with_inverse):
    count, n, _ = a.shape
    shape = jax.ShapeDtypeStruct((count, n, n), jnp.float32)
    vmem = pl.BlockSpec(memory_space=pltpu.VMEM)
    scratch = [pltpu.VMEM((count, n, n), jnp.float32)] * (2 if with_inverse else 1)
    return pl.pallas_call(
        functools.partial(_cholesky_body, with_inverse),
        out_shape=(shape, shape) if with_inverse else shape,
        in_specs=[vmem],
        out_specs=(vmem, vmem) if with_inverse else vmem,
        scratch_shapes=scratch,
    )(a)


GROUP = 8
BLOCK = 256


def _sketch_body(flag_ref, rows_ref, points_ref, omega_ref, sketch_ref, tile):
    step = pl.program_id(0)
    groups = BLOCK // GROUP
    point_x = points_ref[0:1, :]
    point_y = points_ref[1:2, :]
    point_z = points_ref[2:3, :]
    for group in range(groups):
        span = slice(group * GROUP, (group + 1) * GROUP)
        live = flag_ref[step * groups + group] > 0

        @pl.when(live)
        def _():
            row_data = rows_ref[span, :]
            delta_x = row_data[:, 0:1] - point_x
            delta_y = row_data[:, 1:2] - point_y
            delta_z = row_data[:, 2:3] - point_z
            distance = delta_x * delta_x + delta_y * delta_y + delta_z * delta_z
            tile[span, :] = (row_data[:, 3:4] * lax.rsqrt(distance + 0.0009)).astype(jnp.bfloat16)

        @pl.when(jnp.logical_not(live))
        def _():
            tile[span, :] = jnp.zeros((GROUP, tile.shape[1]), jnp.bfloat16)

    sketch_ref[...] = jnp.dot(tile[...], omega_ref[...], preferred_element_type=jnp.float32)


def sketch_rows(received, points, omega_full):
    slots = received.shape[1]
    rows = received.T
    flags = jnp.any(rows[:, 3].reshape(slots // GROUP, GROUP) != 0, axis=1).astype(jnp.int32)
    proxies = points.shape[1]
    rank = omega_full.shape[1]
    return pl.pallas_call(
        _sketch_body,
        out_shape=jax.ShapeDtypeStruct((slots, rank), jnp.float32),
        grid=(slots // BLOCK,),
        in_specs=[
            pl.BlockSpec(memory_space=pltpu.SMEM),
            pl.BlockSpec((BLOCK, 4), lambda i: (i, 0)),
            pl.BlockSpec((3, proxies), lambda i: (0, 0)),
            pl.BlockSpec((proxies, rank), lambda i: (0, 0)),
        ],
        out_specs=pl.BlockSpec((BLOCK, rank), lambda i: (i, 0)),
        scratch_shapes=[pltpu.VMEM((BLOCK, proxies), jnp.bfloat16)],
        cost_estimate=pl.CostEstimate(
            flops=2 * slots * proxies * rank + 12 * slots * proxies,
            transcendentals=slots * proxies,
            bytes_accessed=slots * 16 + proxies * rank * 2 + slots * rank * 4,
        ),
    )(flags, rows, points, omega_full)


def per_device(panels, panel_dest, proxy_pool, proxy_index, omega, merge_maps):
    highest = lax.Precision.HIGHEST
    device_count = lax.axis_size(("leaf", "blk"))
    blk_count = lax.axis_size("blk")
    leaf_count = lax.axis_size("leaf")
    blk_index = lax.axis_index("blk")
    own_panels = panels.shape[1]
    capacity = 2 * own_panels // device_count
    rank_width = omega.shape[2]
    identity = jnp.eye(rank_width, dtype=jnp.float32)
    omega_parts = [omega[0]] + [from_shift(omega[0], "blk", shift) for shift in range(1, blk_count)]
    destination = panel_dest[:, 0]
    one_hot = (destination[:, None] == jnp.arange(device_count, dtype=jnp.int32)[None, :]).astype(
        jnp.int32
    )
    running = jnp.cumsum(one_hot, axis=0)
    slot_index = jnp.sum(running * one_hot, axis=1) - 1
    position = destination * capacity + slot_index
    outgoing = jnp.zeros((4, device_count * capacity), jnp.float32).at[:, position].set(panels)
    received = lax.all_to_all(outgoing, ("leaf", "blk"), split_axis=1, concat_axis=1, tiled=True)
    chunk = omega.shape[1]
    leaf_proxies = jnp.concatenate(
        [
            lax.dynamic_slice_in_dim(proxy_index[0], ((blk_index - shift) % blk_count) * chunk, chunk)
            for shift in range(blk_count)
        ]
    )
    points = jnp.take(proxy_pool, leaf_proxies, axis=1)
    sketch = sketch_rows(received, points, jnp.concatenate(omega_parts, axis=0))
    leaf_index = lax.axis_index("leaf")
    levels = leaf_count.bit_length() - 1
    path = []
    for level_index in range(levels):
        heap_index = (leaf_count >> level_index) + (leaf_index >> level_index)
        node_map = lax.dynamic_index_in_dim(merge_maps, heap_index - 2, 0, keepdims=False)
        path.append(node_map if not path else jnp.dot(path[-1], node_map, precision=highest))
    path = jnp.stack(path, axis=0)
    gram_part = jnp.dot(sketch.T, sketch, precision=highest)
    gram_sum = gram_part + from_partner(gram_part, "blk", 0)
    gram_sum = gram_sum + from_partner(gram_sum, "blk", 1)
    gram_full = gram_sum / (own_panels * blk_count) + identity
    mapped = jnp.einsum("ij,kjm->kim", gram_full, path, precision=highest)
    terms = jnp.einsum("kji,kjm->kim", path, mapped, precision=highest)
    for level_index in range(levels):
        upper = terms[level_index:]
        upper = upper + from_partner(upper, "leaf", level_index)
        terms = jnp.concatenate([terms[:level_index], upper], axis=0) if level_index else upper
    scales = jnp.asarray([0.5 ** (level_index + 1) for level_index in range(levels)], jnp.float32)
    ancestor_grams = terms * scales[:, None, None]
    lower_factor, lower_inverse = cholesky_batch(gram_full[None], True)
    basis_rows = jnp.dot(sketch, lower_inverse[0].T, precision=highest)
    returned = lax.all_to_all(
        basis_rows.astype(jnp.bfloat16), ("leaf", "blk"), split_axis=0, concat_axis=0, tiled=True
    )
    leaf_basis = jnp.take(returned, position, axis=0).astype(jnp.float32).T
    ancestor_factor = cholesky_batch(ancestor_grams, False)
    return (leaf_basis, lower_factor, ancestor_factor[None])


def solution(mesh):
    placed = (
        P(None, ("leaf", "blk")),
        P(("leaf", "blk"), None),
        P(),
        P("leaf", None),
        P("leaf", "blk", None),
        P(),
    )
    return jax.shard_map(
        per_device,
        mesh=mesh,
        in_specs=placed,
        out_specs=(P(None, ("leaf", "blk")), P("leaf", None, None), P("leaf", None, None, None)),
        check_vma=False,
    )
```

```python
import functools

import jax
import jax.numpy as jnp
from jax import lax
from jax.experimental import pallas as pl
from jax.experimental.pallas import tpu as pltpu
from jax.sharding import PartitionSpec as P


def from_partner(value, axis, bit):
    mask = 2**bit
    pairs = [(source, source ^ mask) for source in range(lax.axis_size(axis))]
    return lax.ppermute(value, axis, pairs)


def from_shift(value, axis, shift):
    size = lax.axis_size(axis)
    pairs = [(source, (source + shift) % size) for source in range(size)]
    return lax.ppermute(value, axis, pairs)


def kernel_tile(row_data, points):
    delta_x = row_data[0][:, None] - points[0][None, :]
    delta_y = row_data[1][:, None] - points[1][None, :]
    delta_z = row_data[2][:, None] - points[2][None, :]
    distance = delta_x * delta_x + delta_y * delta_y + delta_z * delta_z
    return (row_data[3][:, None] * lax.rsqrt(distance + 0.0009)).astype(jnp.bfloat16)


def _cholesky_body(with_inverse, a_ref, l_ref, *rest):
    if with_inverse:
        inv_ref, work, inverse_work = rest
    else:
        (work,) = rest
    count, n, _ = a_ref.shape
    rows = lax.broadcasted_iota(jnp.int32, (n, n), 0)
    cols = lax.broadcasted_iota(jnp.int32, (n, n), 1)
    work[...] = a_ref[...]
    if with_inverse:
        eye = jnp.where(rows == cols, 1.0, 0.0).astype(jnp.float32)
        for b in range(count):
            inverse_work[b] = eye
    for j in range(n):
        top = (j // 8) * 8
        sub = lax.broadcasted_iota(jnp.int32, (n - top, 1), 0) + top
        for b in range(count):
            block = work[b, top:, :]
            row = work[b, j:j + 1, :]
            pivot = row[:, j:j + 1]
            scale = lax.rsqrt(pivot)
            factor = jnp.where(sub > j, block[:, j:j + 1] * (1.0 / pivot), 0.0)
            work[b, top:, :] = jnp.where(sub == j, row * scale, block - factor * row)
            if with_inverse:
                inverse_block = inverse_work[b, top:, :]
                inverse_row = inverse_work[b, j:j + 1, :]
                inverse_work[b, top:, :] = jnp.where(
                    sub == j, inverse_row * scale, inverse_block - factor * inverse_row
                )
    for b in range(count):
        l_ref[b] = jnp.transpose(jnp.where(cols >= rows, work[b], 0.0))
        if with_inverse:
            inv_ref[b] = jnp.where(cols <= rows, inverse_work[b], 0.0)


def cholesky_batch(a, with_inverse):
    count, n, _ = a.shape
    shape = jax.ShapeDtypeStruct((count, n, n), jnp.float32)
    vmem = pl.BlockSpec(memory_space=pltpu.VMEM)
    scratch = [pltpu.VMEM((count, n, n), jnp.float32)] * (2 if with_inverse else 1)
    return pl.pallas_call(
        functools.partial(_cholesky_body, with_inverse),
        out_shape=(shape, shape) if with_inverse else shape,
        in_specs=[vmem],
        out_specs=(vmem, vmem) if with_inverse else vmem,
        scratch_shapes=scratch,
    )(a)


def per_device(panels, panel_dest, proxy_pool, proxy_index, omega, merge_maps):
    highest = lax.Precision.HIGHEST
    device_count = lax.axis_size(("leaf", "blk"))
    blk_count = lax.axis_size("blk")
    leaf_count = lax.axis_size("leaf")
    blk_index = lax.axis_index("blk")
    own_panels = panels.shape[1]
    capacity = 2 * own_panels // device_count
    rank_width = omega.shape[2]
    identity = jnp.eye(rank_width, dtype=jnp.float32)
    omega_parts = [omega[0]] + [from_shift(omega[0], "blk", shift) for shift in range(1, blk_count)]
    destination = panel_dest[:, 0]
    one_hot = (destination[:, None] == jnp.arange(device_count, dtype=jnp.int32)[None, :]).astype(
        jnp.int32
    )
    running = jnp.cumsum(one_hot, axis=0)
    slot_index = jnp.sum(running * one_hot, axis=1) - 1
    position = destination * capacity + slot_index
    outgoing = jnp.zeros((4, device_count * capacity), jnp.float32).at[:, position].set(panels)
    received = lax.all_to_all(outgoing, ("leaf", "blk"), split_axis=1, concat_axis=1, tiled=True)
    chunk = omega.shape[1]
    leaf_proxies = jnp.concatenate(
        [
            lax.dynamic_slice_in_dim(proxy_index[0], ((blk_index - shift) % blk_count) * chunk, chunk)
            for shift in range(blk_count)
        ]
    )
    points = jnp.take(proxy_pool, leaf_proxies, axis=1)
    tile = kernel_tile(received, points)
    sketch = jnp.dot(tile, jnp.concatenate(omega_parts, axis=0), preferred_element_type=jnp.float32)
    leaf_index = lax.axis_index("leaf")
    levels = leaf_count.bit_length() - 1
    path = []
    for level_index in range(levels):
        heap_index = (leaf_count >> level_index) + (leaf_index >> level_index)
        node_map = lax.dynamic_index_in_dim(merge_maps, heap_index - 2, 0, keepdims=False)
        path.append(node_map if not path else jnp.dot(path[-1], node_map, precision=highest))
    path = jnp.stack(path, axis=0)
    gram_part = jnp.dot(sketch.T, sketch, precision=highest)
    gram_parts = lax.all_gather(gram_part, "blk", axis=0)
    gram_sum = (gram_parts[0] + gram_parts[1]) + (gram_parts[2] + gram_parts[3])
    gram_full = gram_sum / (own_panels * blk_count) + identity
    mapped = jnp.einsum("ij,kjm->kim", gram_full, path, precision=highest)
    terms = jnp.einsum("kji,kjm->kim", path, mapped, precision=highest)
    for level_index in range(levels):
        upper = terms[level_index:]
        upper = upper + from_partner(upper, "leaf", level_index)
        terms = jnp.concatenate([terms[:level_index], upper], axis=0) if level_index else upper
    scales = jnp.asarray([0.5 ** (level_index + 1) for level_index in range(levels)], jnp.float32)
    ancestor_grams = terms * scales[:, None, None]
    lower_factor, lower_inverse = cholesky_batch(gram_full[None], True)
    basis_rows = jnp.dot(sketch, lower_inverse[0].T, precision=highest)
    returned = lax.all_to_all(
        basis_rows.astype(jnp.bfloat16), ("leaf", "blk"), split_axis=0, concat_axis=0, tiled=True
    )
    leaf_basis = jnp.take(returned.astype(jnp.float32), position, axis=0).T
    ancestor_factor = cholesky_batch(ancestor_grams, False)
    return (leaf_basis, lower_factor, ancestor_factor[None])


def solution(mesh):
    placed = (
        P(None, ("leaf", "blk")),
        P(("leaf", "blk"), None),
        P(),
        P("leaf", None),
        P("leaf", "blk", None),
        P(),
    )
    return jax.shard_map(
        per_device,
        mesh=mesh,
        in_specs=placed,
        out_specs=(P(None, ("leaf", "blk")), P("leaf", None, None), P("leaf", None, None, None)),
        check_vma=False,
    )
```

```python
import functools

import jax
import jax.numpy as jnp
from jax import lax
from jax.experimental import pallas as pl
from jax.experimental.pallas import tpu as pltpu
from jax.sharding import PartitionSpec as P


def from_partner(value, axis, bit):
    mask = 2**bit
    pairs = [(source, source ^ mask) for source in range(lax.axis_size(axis))]
    return lax.ppermute(value, axis, pairs)


def from_shift(value, axis, shift):
    size = lax.axis_size(axis)
    pairs = [(source, (source + shift) % size) for source in range(size)]
    return lax.ppermute(value, axis, pairs)


def kernel_tile(row_data, points):
    delta_x = row_data[0][:, None] - points[0][None, :]
    delta_y = row_data[1][:, None] - points[1][None, :]
    delta_z = row_data[2][:, None] - points[2][None, :]
    distance = delta_x * delta_x + delta_y * delta_y + delta_z * delta_z
    return (row_data[3][:, None] * lax.rsqrt(distance + 0.0009)).astype(jnp.bfloat16)


def _cholesky_body(with_inverse, a_ref, l_ref, *rest):
    if with_inverse:
        inv_ref, work, inverse_work = rest
    else:
        (work,) = rest
    count, n, _ = a_ref.shape
    rows = lax.broadcasted_iota(jnp.int32, (n, n), 0)
    cols = lax.broadcasted_iota(jnp.int32, (n, n), 1)
    work[...] = a_ref[...]
    if with_inverse:
        eye = jnp.where(rows == cols, 1.0, 0.0).astype(jnp.float32)
        for b in range(count):
            inverse_work[b] = eye
    for j in range(n):
        top = (j // 8) * 8
        sub = lax.broadcasted_iota(jnp.int32, (n - top, 1), 0) + top
        for b in range(count):
            block = work[b, top:, :]
            row = work[b, j:j + 1, :]
            pivot = row[:, j:j + 1]
            scale = lax.rsqrt(pivot)
            factor = jnp.where(sub > j, block[:, j:j + 1] * (1.0 / pivot), 0.0)
            work[b, top:, :] = jnp.where(sub == j, row * scale, block - factor * row)
            if with_inverse:
                inverse_block = inverse_work[b, top:, :]
                inverse_row = inverse_work[b, j:j + 1, :]
                inverse_work[b, top:, :] = jnp.where(
                    sub == j, inverse_row * scale, inverse_block - factor * inverse_row
                )
    for b in range(count):
        l_ref[b] = jnp.transpose(jnp.where(cols >= rows, work[b], 0.0))
        if with_inverse:
            inv_ref[b] = jnp.where(cols <= rows, inverse_work[b], 0.0)


def cholesky_batch(a, with_inverse):
    count, n, _ = a.shape
    shape = jax.ShapeDtypeStruct((count, n, n), jnp.float32)
    vmem = pl.BlockSpec(memory_space=pltpu.VMEM)
    scratch = [pltpu.VMEM((count, n, n), jnp.float32)] * (2 if with_inverse else 1)
    return pl.pallas_call(
        functools.partial(_cholesky_body, with_inverse),
        out_shape=(shape, shape) if with_inverse else shape,
        in_specs=[vmem],
        out_specs=(vmem, vmem) if with_inverse else vmem,
        scratch_shapes=scratch,
    )(a)


def per_device(panels, panel_dest, proxy_pool, proxy_index, omega, merge_maps):
    highest = lax.Precision.HIGHEST
    device_count = lax.axis_size(("leaf", "blk"))
    blk_count = lax.axis_size("blk")
    leaf_count = lax.axis_size("leaf")
    blk_index = lax.axis_index("blk")
    own_panels = panels.shape[1]
    capacity = 2 * own_panels // device_count
    rank_width = omega.shape[2]
    identity = jnp.eye(rank_width, dtype=jnp.float32)
    omega_parts = [omega[0]] + [from_shift(omega[0], "blk", shift) for shift in range(1, blk_count)]
    destination = panel_dest[:, 0] // blk_count
    capacity = blk_count * capacity
    one_hot = (destination[:, None] == jnp.arange(device_count, dtype=jnp.int32)[None, :]).astype(
        jnp.int32
    )
    running = jnp.cumsum(one_hot, axis=0)
    slot_index = jnp.sum(running * one_hot, axis=1) - 1
    position = destination * capacity + slot_index
    outgoing = jnp.zeros((4, leaf_count * capacity), jnp.float32).at[:, position].set(panels)
    outgoing = jnp.transpose(outgoing.reshape(4, leaf_count, capacity), (1, 0, 2))
    received = lax.all_to_all(outgoing, "leaf", split_axis=0, concat_axis=0, tiled=True)
    received = jnp.transpose(received, (1, 0, 2)).reshape(4, leaf_count * capacity)
    chunk = omega.shape[1]
    leaf_proxies = jnp.concatenate(
        [
            lax.dynamic_slice_in_dim(proxy_index[0], ((blk_index - shift) % blk_count) * chunk, chunk)
            for shift in range(blk_count)
        ]
    )
    points = jnp.take(proxy_pool, leaf_proxies, axis=1)
    tile = kernel_tile(received, points)
    sketch = jnp.dot(tile, jnp.concatenate(omega_parts, axis=0), preferred_element_type=jnp.float32)
    leaf_index = lax.axis_index("leaf")
    levels = leaf_count.bit_length() - 1
    path = []
    for level_index in range(levels):
        heap_index = (leaf_count >> level_index) + (leaf_index >> level_index)
        node_map = lax.dynamic_index_in_dim(merge_maps, heap_index - 2, 0, keepdims=False)
        path.append(node_map if not path else jnp.dot(path[-1], node_map, precision=highest))
    path = jnp.stack(path, axis=0)
    gram_part = jnp.dot(sketch.T, sketch, precision=highest)
    gram_sum = gram_part + from_partner(gram_part, "blk", 0)
    gram_sum = gram_sum + from_partner(gram_sum, "blk", 1)
    gram_full = gram_sum / (own_panels * blk_count) + identity
    mapped = jnp.einsum("ij,kjm->kim", gram_full, path, precision=highest)
    terms = jnp.einsum("kji,kjm->kim", path, mapped, precision=highest)
    for level_index in range(levels):
        upper = terms[level_index:]
        upper = upper + from_partner(upper, "leaf", level_index)
        terms = jnp.concatenate([terms[:level_index], upper], axis=0) if level_index else upper
    scales = jnp.asarray([0.5 ** (level_index + 1) for level_index in range(levels)], jnp.float32)
    ancestor_grams = terms * scales[:, None, None]
    lower_factor, lower_inverse = cholesky_batch(gram_full[None], True)
    basis_rows = jnp.dot(sketch, lower_inverse[0].T, precision=highest)
    returned = lax.all_to_all(
        basis_rows.astype(jnp.bfloat16), "leaf", split_axis=0, concat_axis=0, tiled=True
    )
    leaf_basis = jnp.take(returned.astype(jnp.float32), position, axis=0).T
    ancestor_factor = cholesky_batch(ancestor_grams, False)
    return (leaf_basis, lower_factor, ancestor_factor[None])


def solution(mesh):
    placed = (
        P(None, ("leaf", "blk")),
        P(("leaf", "blk"), None),
        P(),
        P("leaf", None),
        P("leaf", "blk", None),
        P(),
    )
    return jax.shard_map(
        per_device,
        mesh=mesh,
        in_specs=placed,
        out_specs=(P(None, ("leaf", "blk")), P("leaf", None, None), P("leaf", None, None, None)),
        check_vma=False,
    )
```

```python
import functools

import jax
import jax.numpy as jnp
from jax import lax
from jax.experimental import pallas as pl
from jax.experimental.pallas import tpu as pltpu
from jax.sharding import PartitionSpec as P


def from_partner(value, axis, bit):
    mask = 2**bit
    pairs = [(source, source ^ mask) for source in range(lax.axis_size(axis))]
    return lax.ppermute(value, axis, pairs)


def from_shift(value, axis, shift):
    size = lax.axis_size(axis)
    pairs = [(source, (source + shift) % size) for source in range(size)]
    return lax.ppermute(value, axis, pairs)


def kernel_tile(row_data, points):
    delta_x = row_data[0][:, None] - points[0][None, :]
    delta_y = row_data[1][:, None] - points[1][None, :]
    delta_z = row_data[2][:, None] - points[2][None, :]
    distance = delta_x * delta_x + delta_y * delta_y + delta_z * delta_z
    return (row_data[3][:, None] * lax.rsqrt(distance + 0.0009)).astype(jnp.bfloat16)


def _cholesky_body(with_inverse, a_ref, l_ref, *rest):
    if with_inverse:
        inv_ref, work, inverse_work = rest
    else:
        (work,) = rest
    count, n, _ = a_ref.shape
    rows = lax.broadcasted_iota(jnp.int32, (n, n), 0)
    cols = lax.broadcasted_iota(jnp.int32, (n, n), 1)
    work[...] = a_ref[...]
    if with_inverse:
        eye = jnp.where(rows == cols, 1.0, 0.0).astype(jnp.float32)
        for b in range(count):
            inverse_work[b] = eye
    for j in range(n):
        top = (j // 8) * 8
        sub = lax.broadcasted_iota(jnp.int32, (n - top, 1), 0) + top
        for b in range(count):
            block = work[b, top:, :]
            row = work[b, j:j + 1, :]
            pivot = row[:, j:j + 1]
            scale = lax.rsqrt(pivot)
            factor = jnp.where(sub > j, block[:, j:j + 1] * (1.0 / pivot), 0.0)
            work[b, top:, :] = jnp.where(sub == j, row * scale, block - factor * row)
            if with_inverse:
                inverse_block = inverse_work[b, top:, :]
                inverse_row = inverse_work[b, j:j + 1, :]
                inverse_work[b, top:, :] = jnp.where(
                    sub == j, inverse_row * scale, inverse_block - factor * inverse_row
                )
    for b in range(count):
        l_ref[b] = jnp.transpose(jnp.where(cols >= rows, work[b], 0.0))
        if with_inverse:
            inv_ref[b] = jnp.where(cols <= rows, inverse_work[b], 0.0)


def cholesky_batch(a, with_inverse):
    count, n, _ = a.shape
    shape = jax.ShapeDtypeStruct((count, n, n), jnp.float32)
    vmem = pl.BlockSpec(memory_space=pltpu.VMEM)
    scratch = [pltpu.VMEM((count, n, n), jnp.float32)] * (2 if with_inverse else 1)
    return pl.pallas_call(
        functools.partial(_cholesky_body, with_inverse),
        out_shape=(shape, shape) if with_inverse else shape,
        in_specs=[vmem],
        out_specs=(vmem, vmem) if with_inverse else vmem,
        scratch_shapes=scratch,
    )(a)


def per_device(panels, panel_dest, proxy_pool, proxy_index, omega, merge_maps):
    highest = lax.Precision.HIGHEST
    device_count = lax.axis_size(("leaf", "blk"))
    blk_count = lax.axis_size("blk")
    leaf_count = lax.axis_size("leaf")
    blk_index = lax.axis_index("blk")
    own_panels = panels.shape[1]
    capacity = 2 * own_panels // device_count
    rank_width = omega.shape[2]
    identity = jnp.eye(rank_width, dtype=jnp.float32)
    omega_parts = [omega[0]] + [from_shift(omega[0], "blk", shift) for shift in range(1, blk_count)]
    destination = panel_dest[:, 0] // blk_count
    capacity = blk_count * capacity
    one_hot = (destination[:, None] == jnp.arange(device_count, dtype=jnp.int32)[None, :]).astype(
        jnp.int32
    )
    running = jnp.cumsum(one_hot, axis=0)
    slot_index = jnp.sum(running * one_hot, axis=1) - 1
    position = destination * capacity + slot_index
    outgoing = jnp.zeros((4, leaf_count * capacity), jnp.float32).at[:, position].set(panels)
    outgoing = jnp.transpose(outgoing.reshape(4, leaf_count, capacity), (1, 0, 2))
    received = lax.all_to_all(outgoing, "leaf", split_axis=0, concat_axis=0, tiled=True)
    received = jnp.transpose(received, (1, 0, 2)).reshape(4, leaf_count * capacity)
    chunk = omega.shape[1]
    leaf_proxies = jnp.concatenate(
        [
            lax.dynamic_slice_in_dim(proxy_index[0], ((blk_index - shift) % blk_count) * chunk, chunk)
            for shift in range(blk_count)
        ]
    )
    points = jnp.take(proxy_pool, leaf_proxies, axis=1)
    tile = kernel_tile(received, points)
    sketch = jnp.dot(tile, jnp.concatenate(omega_parts, axis=0), preferred_element_type=jnp.float32)
    leaf_index = lax.axis_index("leaf")
    levels = leaf_count.bit_length() - 1
    path = []
    for level_index in range(levels):
        heap_index = (leaf_count >> level_index) + (leaf_index >> level_index)
        node_map = lax.dynamic_index_in_dim(merge_maps, heap_index - 2, 0, keepdims=False)
        path.append(node_map if not path else jnp.dot(path[-1], node_map, precision=highest))
    path = jnp.stack(path, axis=0)
    gram_part = jnp.dot(sketch.T, sketch, precision=highest)
    gram_sum = gram_part + from_partner(gram_part, "blk", 0)
    gram_sum = gram_sum + from_partner(gram_sum, "blk", 1)
    gram_full = gram_sum / (own_panels * blk_count) + identity
    mapped = jnp.einsum("ij,kjm->kim", gram_full, path, precision=highest)
    terms = jnp.einsum("kji,kjm->kim", path, mapped, precision=highest)
    for level_index in range(levels):
        upper = terms[level_index:]
        upper = upper + from_partner(upper, "leaf", level_index)
        terms = jnp.concatenate([terms[:level_index], upper], axis=0) if level_index else upper
    scales = jnp.asarray([0.5 ** (level_index + 1) for level_index in range(levels)], jnp.float32)
    ancestor_grams = terms * scales[:, None, None]
    lower_factor, lower_inverse = cholesky_batch(gram_full[None], True)
    basis_rows = jnp.dot(sketch, lower_inverse[0].T, precision=highest)
    returned = lax.all_to_all(
        basis_rows.astype(jnp.bfloat16), "leaf", split_axis=0, concat_axis=0, tiled=True
    )
    leaf_basis = jnp.take(returned, position, axis=0).astype(jnp.float32).T
    ancestor_factor = cholesky_batch(ancestor_grams, False)
    return (leaf_basis, lower_factor, ancestor_factor[None])


def solution(mesh):
    placed = (
        P(None, ("leaf", "blk")),
        P(("leaf", "blk"), None),
        P(),
        P("leaf", None),
        P("leaf", "blk", None),
        P(),
    )
    return jax.shard_map(
        per_device,
        mesh=mesh,
        in_specs=placed,
        out_specs=(P(None, ("leaf", "blk")), P("leaf", None, None), P("leaf", None, None, None)),
        check_vma=False,
    )
```

```python
import functools

import jax
import jax.numpy as jnp
from jax import lax
from jax.experimental import pallas as pl
from jax.experimental.pallas import tpu as pltpu
from jax.sharding import PartitionSpec as P


def from_partner(value, axis, bit):
    mask = 2**bit
    pairs = [(source, source ^ mask) for source in range(lax.axis_size(axis))]
    return lax.ppermute(value, axis, pairs)


def from_shift(value, axis, shift):
    size = lax.axis_size(axis)
    pairs = [(source, (source + shift) % size) for source in range(size)]
    return lax.ppermute(value, axis, pairs)


def kernel_tile(row_data, points):
    delta_x = row_data[0][:, None] - points[0][None, :]
    delta_y = row_data[1][:, None] - points[1][None, :]
    delta_z = row_data[2][:, None] - points[2][None, :]
    distance = delta_x * delta_x + delta_y * delta_y + delta_z * delta_z
    return (row_data[3][:, None] * lax.rsqrt(distance + 0.0009)).astype(jnp.bfloat16)


def _cholesky_body(with_inverse, a_ref, l_ref, *rest):
    if with_inverse:
        inv_ref, work, inverse_work = rest
    else:
        (work,) = rest
    count, n, _ = a_ref.shape
    rows = lax.broadcasted_iota(jnp.int32, (n, n), 0)
    cols = lax.broadcasted_iota(jnp.int32, (n, n), 1)
    work[...] = a_ref[...]
    if with_inverse:
        eye = jnp.where(rows == cols, 1.0, 0.0).astype(jnp.float32)
        for b in range(count):
            inverse_work[b] = eye
    for j in range(n):
        top = (j // 8) * 8
        sub = lax.broadcasted_iota(jnp.int32, (n - top, 1), 0) + top
        for b in range(count):
            block = work[b, top:, :]
            row = work[b, j:j + 1, :]
            pivot = row[:, j:j + 1]
            scale = lax.rsqrt(pivot)
            factor = jnp.where(sub > j, block[:, j:j + 1] * (1.0 / pivot), 0.0)
            work[b, top:, :] = jnp.where(sub == j, row * scale, block - factor * row)
            if with_inverse:
                inverse_block = inverse_work[b, top:, :]
                inverse_row = inverse_work[b, j:j + 1, :]
                inverse_work[b, top:, :] = jnp.where(
                    sub == j, inverse_row * scale, inverse_block - factor * inverse_row
                )
    for b in range(count):
        l_ref[b] = jnp.transpose(jnp.where(cols >= rows, work[b], 0.0))
        if with_inverse:
            inv_ref[b] = jnp.where(cols <= rows, inverse_work[b], 0.0)


def cholesky_batch(a, with_inverse):
    count, n, _ = a.shape
    shape = jax.ShapeDtypeStruct((count, n, n), jnp.float32)
    vmem = pl.BlockSpec(memory_space=pltpu.VMEM)
    scratch = [pltpu.VMEM((count, n, n), jnp.float32)] * (2 if with_inverse else 1)
    return pl.pallas_call(
        functools.partial(_cholesky_body, with_inverse),
        out_shape=(shape, shape) if with_inverse else shape,
        in_specs=[vmem],
        out_specs=(vmem, vmem) if with_inverse else vmem,
        scratch_shapes=scratch,
    )(a)


def per_device(panels, panel_dest, proxy_pool, proxy_index, omega, merge_maps):
    highest = lax.Precision.HIGHEST
    device_count = lax.axis_size(("leaf", "blk"))
    blk_count = lax.axis_size("blk")
    leaf_count = lax.axis_size("leaf")
    blk_index = lax.axis_index("blk")
    own_panels = panels.shape[1]
    capacity = 2 * own_panels // device_count
    rank_width = omega.shape[2]
    identity = jnp.eye(rank_width, dtype=jnp.float32)
    omega_parts = [omega[0]] + [from_shift(omega[0], "blk", shift) for shift in range(1, blk_count)]
    destination = panel_dest[:, 0] // blk_count
    capacity = blk_count * capacity
    one_hot = (destination[:, None] == jnp.arange(device_count, dtype=jnp.int32)[None, :]).astype(
        jnp.int32
    )
    running = jnp.cumsum(one_hot, axis=0)
    slot_index = jnp.sum(running * one_hot, axis=1) - 1
    position = destination * capacity + slot_index
    outgoing = jnp.zeros((4, leaf_count * capacity), jnp.float32).at[:, position].set(panels)
    outgoing = jnp.transpose(outgoing.reshape(4, leaf_count, capacity), (1, 0, 2))
    received = lax.all_to_all(outgoing, "leaf", split_axis=0, concat_axis=0, tiled=True)
    received = jnp.transpose(received, (1, 0, 2)).reshape(4, leaf_count * capacity)
    chunk = omega.shape[1]
    leaf_proxies = jnp.concatenate(
        [
            lax.dynamic_slice_in_dim(proxy_index[0], ((blk_index - shift) % blk_count) * chunk, chunk)
            for shift in range(blk_count)
        ]
    )
    points = jnp.take(proxy_pool, leaf_proxies, axis=1)
    tile = kernel_tile(received, points)
    sketch = jnp.dot(tile, jnp.concatenate(omega_parts, axis=0), preferred_element_type=jnp.float32)
    leaf_index = lax.axis_index("leaf")
    levels = leaf_count.bit_length() - 1
    path = []
    for level_index in range(levels):
        heap_index = (leaf_count >> level_index) + (leaf_index >> level_index)
        node_map = lax.dynamic_index_in_dim(merge_maps, heap_index - 2, 0, keepdims=False)
        path.append(node_map if not path else jnp.dot(path[-1], node_map, precision=highest))
    path = jnp.stack(path, axis=0)
    gram_part = jnp.dot(sketch.T, sketch, precision=highest)
    gram_sum = gram_part + from_partner(gram_part, "blk", 0)
    gram_sum = gram_sum + from_partner(gram_sum, "blk", 1)
    gram_full = gram_sum / (own_panels * blk_count) + identity
    mapped = jnp.einsum("ij,kjm->kim", gram_full, path, precision=highest)
    terms = jnp.einsum("kji,kjm->kim", path, mapped, precision=highest)
    scales = [0.5 ** (level_index + 1) for level_index in range(levels)]
    ready = {levels // 2: 0, levels - 2: levels // 2 + 1, levels - 1: levels - 1}
    factor_parts = []
    for level_index in range(levels):
        upper = terms[level_index:]
        upper = upper + from_partner(upper, "leaf", level_index)
        terms = jnp.concatenate([terms[:level_index], upper], axis=0) if level_index else upper
        if level_index in ready:
            first = ready[level_index]
            grams = terms[first:level_index + 1] * jnp.asarray(
                scales[first:level_index + 1], jnp.float32
            )[:, None, None]
            factor_parts.append(cholesky_batch(grams, False))
    lower_factor, lower_inverse = cholesky_batch(gram_full[None], True)
    basis_rows = jnp.dot(sketch, lower_inverse[0].T, precision=highest)
    returned = lax.all_to_all(
        basis_rows.astype(jnp.bfloat16), "leaf", split_axis=0, concat_axis=0, tiled=True
    )
    leaf_basis = jnp.take(returned, position, axis=0).astype(jnp.float32).T
    ancestor_factor = jnp.concatenate(factor_parts, axis=0)
    return (leaf_basis, lower_factor, ancestor_factor[None])


def solution(mesh):
    placed = (
        P(None, ("leaf", "blk")),
        P(("leaf", "blk"), None),
        P(),
        P("leaf", None),
        P("leaf", "blk", None),
        P(),
    )
    return jax.shard_map(
        per_device,
        mesh=mesh,
        in_specs=placed,
        out_specs=(P(None, ("leaf", "blk")), P("leaf", None, None), P("leaf", None, None, None)),
        check_vma=False,
    )
```

```python
import functools

import jax
import jax.numpy as jnp
from jax import lax
from jax.experimental import pallas as pl
from jax.experimental.pallas import tpu as pltpu
from jax.sharding import PartitionSpec as P


def from_partner(value, axis, bit):
    mask = 2**bit
    pairs = [(source, source ^ mask) for source in range(lax.axis_size(axis))]
    return lax.ppermute(value, axis, pairs)


def from_shift(value, axis, shift):
    size = lax.axis_size(axis)
    pairs = [(source, (source + shift) % size) for source in range(size)]
    return lax.ppermute(value, axis, pairs)


def kernel_tile(row_data, points):
    delta_x = row_data[0][:, None] - points[0][None, :]
    delta_y = row_data[1][:, None] - points[1][None, :]
    delta_z = row_data[2][:, None] - points[2][None, :]
    distance = delta_x * delta_x + delta_y * delta_y + delta_z * delta_z
    return (row_data[3][:, None] * lax.rsqrt(distance + 0.0009)).astype(jnp.bfloat16)


def _cholesky_body(with_inverse, a_ref, l_ref, *rest):
    if with_inverse:
        inv_ref, work, inverse_work = rest
    else:
        (work,) = rest
    count, n, _ = a_ref.shape
    rows = lax.broadcasted_iota(jnp.int32, (n, n), 0)
    cols = lax.broadcasted_iota(jnp.int32, (n, n), 1)
    work[...] = a_ref[...]
    if with_inverse:
        eye = jnp.where(rows == cols, 1.0, 0.0).astype(jnp.float32)
        for b in range(count):
            inverse_work[b] = eye
    for j in range(n):
        top = (j // 8) * 8
        sub = lax.broadcasted_iota(jnp.int32, (n - top, 1), 0) + top
        for b in range(count):
            block = work[b, top:, :]
            row = work[b, j:j + 1, :]
            pivot = row[:, j:j + 1]
            scale = lax.rsqrt(pivot)
            factor = jnp.where(sub > j, block[:, j:j + 1] * (1.0 / pivot), 0.0)
            work[b, top:, :] = jnp.where(sub == j, row * scale, block - factor * row)
            if with_inverse:
                inverse_block = inverse_work[b, top:, :]
                inverse_row = inverse_work[b, j:j + 1, :]
                inverse_work[b, top:, :] = jnp.where(
                    sub == j, inverse_row * scale, inverse_block - factor * inverse_row
                )
    for b in range(count):
        l_ref[b] = jnp.transpose(jnp.where(cols >= rows, work[b], 0.0))
        if with_inverse:
            inv_ref[b] = jnp.where(cols <= rows, inverse_work[b], 0.0)


def cholesky_batch(a, with_inverse):
    count, n, _ = a.shape
    shape = jax.ShapeDtypeStruct((count, n, n), jnp.float32)
    vmem = pl.BlockSpec(memory_space=pltpu.VMEM)
    scratch = [pltpu.VMEM((count, n, n), jnp.float32)] * (2 if with_inverse else 1)
    return pl.pallas_call(
        functools.partial(_cholesky_body, with_inverse),
        out_shape=(shape, shape) if with_inverse else shape,
        in_specs=[vmem],
        out_specs=(vmem, vmem) if with_inverse else vmem,
        scratch_shapes=scratch,
    )(a)


def per_device(panels, panel_dest, proxy_pool, proxy_index, omega, merge_maps):
    highest = lax.Precision.HIGHEST
    device_count = lax.axis_size(("leaf", "blk"))
    blk_count = lax.axis_size("blk")
    leaf_count = lax.axis_size("leaf")
    blk_index = lax.axis_index("blk")
    own_panels = panels.shape[1]
    capacity = 2 * own_panels // device_count
    rank_width = omega.shape[2]
    identity = jnp.eye(rank_width, dtype=jnp.float32)
    omega_parts = [omega[0]] + [from_shift(omega[0], "blk", shift) for shift in range(1, blk_count)]
    destination = panel_dest[:, 0] // blk_count
    capacity = blk_count * capacity
    one_hot = (destination[:, None] == jnp.arange(device_count, dtype=jnp.int32)[None, :]).astype(
        jnp.int32
    )
    running = jnp.cumsum(one_hot, axis=0)
    slot_index = jnp.sum(running * one_hot, axis=1) - 1
    position = destination * capacity + slot_index
    outgoing = jnp.zeros((4, leaf_count * capacity), jnp.float32).at[:, position].set(panels)
    outgoing = jnp.transpose(outgoing.reshape(4, leaf_count, capacity), (1, 0, 2))
    received = lax.all_to_all(outgoing, "leaf", split_axis=0, concat_axis=0, tiled=True)
    received = jnp.transpose(received, (1, 0, 2)).reshape(4, leaf_count * capacity)
    chunk = omega.shape[1]
    leaf_proxies = jnp.concatenate(
        [
            lax.dynamic_slice_in_dim(proxy_index[0], ((blk_index - shift) % blk_count) * chunk, chunk)
            for shift in range(blk_count)
        ]
    )
    points = jnp.stack([jnp.take(proxy_pool[axis], leaf_proxies) for axis in range(3)])
    tile = kernel_tile(received, points)
    sketch = jnp.dot(tile, jnp.concatenate(omega_parts, axis=0), preferred_element_type=jnp.float32)
    leaf_index = lax.axis_index("leaf")
    levels = leaf_count.bit_length() - 1
    path = []
    for level_index in range(levels):
        heap_index = (leaf_count >> level_index) + (leaf_index >> level_index)
        node_map = lax.dynamic_index_in_dim(merge_maps, heap_index - 2, 0, keepdims=False)
        path.append(node_map if not path else jnp.dot(path[-1], node_map, precision=highest))
    path = jnp.stack(path, axis=0)
    gram_part = jnp.dot(sketch.T, sketch, precision=highest)
    gram_sum = gram_part + from_partner(gram_part, "blk", 0)
    gram_sum = gram_sum + from_partner(gram_sum, "blk", 1)
    gram_full = gram_sum / (own_panels * blk_count) + identity
    mapped = jnp.einsum("ij,kjm->kim", gram_full, path, precision=highest)
    terms = jnp.einsum("kji,kjm->kim", path, mapped, precision=highest)
    for level_index in range(levels):
        upper = terms[level_index:]
        upper = upper + from_partner(upper, "leaf", level_index)
        terms = jnp.concatenate([terms[:level_index], upper], axis=0) if level_index else upper
    scales = jnp.asarray([0.5 ** (level_index + 1) for level_index in range(levels)], jnp.float32)
    ancestor_grams = terms * scales[:, None, None]
    lower_factor, lower_inverse = cholesky_batch(gram_full[None], True)
    basis_rows = jnp.dot(sketch, lower_inverse[0].T, precision=highest)
    returned = lax.all_to_all(
        basis_rows.astype(jnp.bfloat16), "leaf", split_axis=0, concat_axis=0, tiled=True
    )
    leaf_basis = jnp.take(returned, position, axis=0).astype(jnp.float32).T
    ancestor_factor = cholesky_batch(ancestor_grams, False)
    return (leaf_basis, lower_factor, ancestor_factor[None])


def solution(mesh):
    placed = (
        P(None, ("leaf", "blk")),
        P(("leaf", "blk"), None),
        P(),
        P("leaf", None),
        P("leaf", "blk", None),
        P(),
    )
    return jax.shard_map(
        per_device,
        mesh=mesh,
        in_specs=placed,
        out_specs=(P(None, ("leaf", "blk")), P("leaf", None, None), P("leaf", None, None, None)),
        check_vma=False,
    )
```

```python
import functools

import jax
import jax.numpy as jnp
from jax import lax
from jax.experimental import pallas as pl
from jax.experimental.pallas import tpu as pltpu
from jax.sharding import PartitionSpec as P


def from_partner(value, axis, bit):
    mask = 2**bit
    pairs = [(source, source ^ mask) for source in range(lax.axis_size(axis))]
    return lax.ppermute(value, axis, pairs)


def from_shift(value, axis, shift):
    size = lax.axis_size(axis)
    pairs = [(source, (source + shift) % size) for source in range(size)]
    return lax.ppermute(value, axis, pairs)


def kernel_tile(row_data, points):
    delta_x = row_data[0][:, None] - points[0][None, :]
    delta_y = row_data[1][:, None] - points[1][None, :]
    delta_z = row_data[2][:, None] - points[2][None, :]
    distance = delta_x * delta_x + delta_y * delta_y + delta_z * delta_z
    return (row_data[3][:, None] * lax.rsqrt(distance + 0.0009)).astype(jnp.bfloat16)


def _cholesky_body(with_inverse, a_ref, l_ref, *rest):
    if with_inverse:
        inv_ref, work, inverse_work = rest
    else:
        (work,) = rest
    count, n, _ = a_ref.shape
    rows = lax.broadcasted_iota(jnp.int32, (n, n), 0)
    cols = lax.broadcasted_iota(jnp.int32, (n, n), 1)
    work[...] = a_ref[...]
    if with_inverse:
        eye = jnp.where(rows == cols, 1.0, 0.0).astype(jnp.float32)
        for b in range(count):
            inverse_work[b] = eye
    for j in range(n):
        top = (j // 8) * 8
        sub = lax.broadcasted_iota(jnp.int32, (n - top, 1), 0) + top
        for b in range(count):
            block = work[b, top:, :]
            row = work[b, j:j + 1, :]
            pivot = row[:, j:j + 1]
            scale = lax.rsqrt(pivot)
            factor = jnp.where(sub > j, block[:, j:j + 1] * (1.0 / pivot), 0.0)
            work[b, top:, :] = jnp.where(sub == j, row * scale, block - factor * row)
            if with_inverse:
                inverse_block = inverse_work[b, top:, :]
                inverse_row = inverse_work[b, j:j + 1, :]
                inverse_work[b, top:, :] = jnp.where(
                    sub == j, inverse_row * scale, inverse_block - factor * inverse_row
                )
    for b in range(count):
        l_ref[b] = jnp.transpose(jnp.where(cols >= rows, work[b], 0.0))
        if with_inverse:
            inv_ref[b] = jnp.where(cols <= rows, inverse_work[b], 0.0)


def cholesky_batch(a, with_inverse):
    count, n, _ = a.shape
    shape = jax.ShapeDtypeStruct((count, n, n), jnp.float32)
    vmem = pl.BlockSpec(memory_space=pltpu.VMEM)
    scratch = [pltpu.VMEM((count, n, n), jnp.float32)] * (2 if with_inverse else 1)
    return pl.pallas_call(
        functools.partial(_cholesky_body, with_inverse),
        out_shape=(shape, shape) if with_inverse else shape,
        in_specs=[vmem],
        out_specs=(vmem, vmem) if with_inverse else vmem,
        scratch_shapes=scratch,
    )(a)


def per_device(panels, panel_dest, proxy_pool, proxy_index, omega, merge_maps):
    highest = lax.Precision.HIGHEST
    device_count = lax.axis_size(("leaf", "blk"))
    blk_count = lax.axis_size("blk")
    leaf_count = lax.axis_size("leaf")
    blk_index = lax.axis_index("blk")
    own_panels = panels.shape[1]
    capacity = 2 * own_panels // device_count
    rank_width = omega.shape[2]
    identity = jnp.eye(rank_width, dtype=jnp.float32)
    omega_parts = [omega[0]] + [from_shift(omega[0], "blk", shift) for shift in range(1, blk_count)]
    destination = panel_dest[:, 0] // blk_count
    capacity = blk_count * capacity
    one_hot = (destination[:, None] == jnp.arange(device_count, dtype=jnp.int32)[None, :]).astype(
        jnp.int32
    )
    running = jnp.cumsum(one_hot, axis=0)
    slot_index = jnp.sum(running * one_hot, axis=1) - 1
    position = destination * capacity + slot_index
    outgoing = jnp.zeros((4, leaf_count * capacity), jnp.float32).at[:, position].set(panels)
    outgoing = jnp.transpose(outgoing.reshape(4, leaf_count, capacity), (1, 0, 2))
    received = lax.all_to_all(outgoing, "leaf", split_axis=0, concat_axis=0, tiled=True)
    received = jnp.transpose(received, (1, 0, 2)).reshape(4, leaf_count * capacity)
    chunk = omega.shape[1]
    leaf_proxies = jnp.concatenate(
        [
            lax.dynamic_slice_in_dim(proxy_index[0], ((blk_index - shift) % blk_count) * chunk, chunk)
            for shift in range(blk_count)
        ]
    )
    points = jnp.take(proxy_pool, leaf_proxies, axis=1)
    tile = kernel_tile(received, points)
    sketch = jnp.dot(tile, jnp.concatenate(omega_parts, axis=0), preferred_element_type=jnp.float32)
    leaf_index = lax.axis_index("leaf")
    levels = leaf_count.bit_length() - 1
    path = []
    for level_index in range(levels):
        heap_index = (leaf_count >> level_index) + (leaf_index >> level_index)
        node_map = lax.dynamic_index_in_dim(merge_maps, heap_index - 2, 0, keepdims=False)
        path.append(node_map if not path else jnp.dot(path[-1], node_map, precision=highest))
    path = jnp.stack(path, axis=0)
    gram_part = jnp.dot(sketch.T, sketch, precision=highest)
    gram_sum = gram_part + from_partner(gram_part, "blk", 0)
    gram_sum = gram_sum + from_partner(gram_sum, "blk", 1)
    gram_full = gram_sum / (own_panels * blk_count) + identity
    mapped = jnp.einsum("ij,kjm->kim", gram_full, path, precision=highest)
    terms = jnp.einsum("kji,kjm->kim", path, mapped, precision=highest)
    lower_factor, lower_inverse = cholesky_batch(gram_full[None], True)
    basis_rows = jnp.dot(sketch, lower_inverse[0].T, precision=highest)
    returned = lax.all_to_all(
        basis_rows.astype(jnp.bfloat16), "leaf", split_axis=0, concat_axis=0, tiled=True
    )
    leaf_basis = jnp.take(returned, position, axis=0).astype(jnp.float32).T
    scales = jnp.asarray([0.5 ** (level_index + 1) for level_index in range(levels)], jnp.float32)
    early_levels = levels - 2
    for level_index in range(levels):
        upper = terms[level_index:]
        received_terms = from_partner(upper, "leaf", level_index)
        if level_index == early_levels:
            early_factor = cholesky_batch(
                terms[:early_levels] * scales[:early_levels, None, None], False
            )
            early_factor, received_terms = lax.optimization_barrier((early_factor, received_terms))
        if level_index == levels - 1:
            leaf_basis, received_terms = lax.optimization_barrier((leaf_basis, received_terms))
        upper = upper + received_terms
        terms = jnp.concatenate([terms[:level_index], upper], axis=0) if level_index else upper
    late_factor = cholesky_batch(terms[early_levels:] * scales[early_levels:, None, None], False)
    ancestor_factor = jnp.concatenate([early_factor, late_factor], axis=0)
    return (leaf_basis, lower_factor, ancestor_factor[None])


def solution(mesh):
    placed = (
        P(None, ("leaf", "blk")),
        P(("leaf", "blk"), None),
        P(),
        P("leaf", None),
        P("leaf", "blk", None),
        P(),
    )
    return jax.shard_map(
        per_device,
        mesh=mesh,
        in_specs=placed,
        out_specs=(P(None, ("leaf", "blk")), P("leaf", None, None), P("leaf", None, None, None)),
        check_vma=False,
    )
```

```python
import functools

import jax
import jax.numpy as jnp
from jax import lax
from jax.experimental import pallas as pl
from jax.experimental.pallas import tpu as pltpu
from jax.sharding import PartitionSpec as P


def from_partner(value, axis, bit):
    mask = 2**bit
    pairs = [(source, source ^ mask) for source in range(lax.axis_size(axis))]
    return lax.ppermute(value, axis, pairs)


def from_shift(value, axis, shift):
    size = lax.axis_size(axis)
    pairs = [(source, (source + shift) % size) for source in range(size)]
    return lax.ppermute(value, axis, pairs)


def kernel_tile(row_data, points):
    delta_x = row_data[0][:, None] - points[0][None, :]
    delta_y = row_data[1][:, None] - points[1][None, :]
    delta_z = row_data[2][:, None] - points[2][None, :]
    distance = delta_x * delta_x + delta_y * delta_y + delta_z * delta_z
    return (row_data[3][:, None] * lax.rsqrt(distance + 0.0009)).astype(jnp.bfloat16)


def _cholesky_body(with_inverse, a_ref, l_ref, *rest):
    if with_inverse:
        inv_ref, work, inverse_work = rest
    else:
        (work,) = rest
    count, n, _ = a_ref.shape
    rows = lax.broadcasted_iota(jnp.int32, (n, n), 0)
    cols = lax.broadcasted_iota(jnp.int32, (n, n), 1)
    work[...] = a_ref[...]
    if with_inverse:
        eye = jnp.where(rows == cols, 1.0, 0.0).astype(jnp.float32)
        for b in range(count):
            inverse_work[b] = eye
    for j in range(n):
        top = (j // 8) * 8
        sub = lax.broadcasted_iota(jnp.int32, (n - top, 1), 0) + top
        for b in range(count):
            block = work[b, top:, :]
            row = work[b, j:j + 1, :]
            pivot = row[:, j:j + 1]
            scale = lax.rsqrt(pivot)
            factor = jnp.where(sub > j, block[:, j:j + 1] * (1.0 / pivot), 0.0)
            work[b, top:, :] = jnp.where(sub == j, row * scale, block - factor * row)
            if with_inverse:
                inverse_block = inverse_work[b, top:, :]
                inverse_row = inverse_work[b, j:j + 1, :]
                inverse_work[b, top:, :] = jnp.where(
                    sub == j, inverse_row * scale, inverse_block - factor * inverse_row
                )
    for b in range(count):
        l_ref[b] = jnp.transpose(jnp.where(cols >= rows, work[b], 0.0))
        if with_inverse:
            inv_ref[b] = jnp.where(cols <= rows, inverse_work[b], 0.0)


def cholesky_batch(a, with_inverse):
    count, n, _ = a.shape
    shape = jax.ShapeDtypeStruct((count, n, n), jnp.float32)
    vmem = pl.BlockSpec(memory_space=pltpu.VMEM)
    scratch = [pltpu.VMEM((count, n, n), jnp.float32)] * (2 if with_inverse else 1)
    return pl.pallas_call(
        functools.partial(_cholesky_body, with_inverse),
        out_shape=(shape, shape) if with_inverse else shape,
        in_specs=[vmem],
        out_specs=(vmem, vmem) if with_inverse else vmem,
        scratch_shapes=scratch,
    )(a)


def per_device(panels, panel_dest, proxy_pool, proxy_index, omega, merge_maps):
    highest = lax.Precision.HIGHEST
    device_count = lax.axis_size(("leaf", "blk"))
    blk_count = lax.axis_size("blk")
    leaf_count = lax.axis_size("leaf")
    blk_index = lax.axis_index("blk")
    own_panels = panels.shape[1]
    capacity = 2 * own_panels // device_count
    rank_width = omega.shape[2]
    identity = jnp.eye(rank_width, dtype=jnp.float32)
    omega_parts = [omega[0]] + [from_shift(omega[0], "blk", shift) for shift in range(1, blk_count)]
    destination = panel_dest[:, 0] // blk_count
    capacity = blk_count * capacity
    one_hot = (destination[:, None] == jnp.arange(device_count, dtype=jnp.int32)[None, :]).astype(
        jnp.int32
    )
    running = jnp.cumsum(one_hot, axis=0)
    slot_index = jnp.sum(running * one_hot, axis=1) - 1
    position = destination * capacity + slot_index
    outgoing = jnp.zeros((4, leaf_count * capacity), jnp.float32).at[:, position].set(panels)
    outgoing = jnp.transpose(outgoing.reshape(4, leaf_count, capacity), (1, 0, 2))
    received = lax.all_to_all(outgoing, "leaf", split_axis=0, concat_axis=0, tiled=True)
    received = jnp.transpose(received, (1, 0, 2)).reshape(4, leaf_count * capacity)
    chunk = omega.shape[1]
    leaf_proxies = jnp.concatenate(
        [
            lax.dynamic_slice_in_dim(proxy_index[0], ((blk_index - shift) % blk_count) * chunk, chunk)
            for shift in range(blk_count)
        ]
    )
    points = jnp.take(proxy_pool, leaf_proxies, axis=1)
    tile = kernel_tile(received, points)
    sketch = jnp.dot(tile, jnp.concatenate(omega_parts, axis=0), preferred_element_type=jnp.float32)
    leaf_index = lax.axis_index("leaf")
    levels = leaf_count.bit_length() - 1
    path = []
    for level_index in range(levels):
        heap_index = (leaf_count >> level_index) + (leaf_index >> level_index)
        node_map = lax.dynamic_index_in_dim(merge_maps, heap_index - 2, 0, keepdims=False)
        path.append(node_map if not path else jnp.dot(path[-1], node_map, precision=highest))
    path = jnp.stack(path, axis=0)
    gram_part = jnp.dot(sketch.T, sketch, precision=highest)
    gram_sum = gram_part + from_partner(gram_part, "blk", 0)
    gram_sum = gram_sum + from_partner(gram_sum, "blk", 1)
    gram_full = gram_sum / (own_panels * blk_count) + identity
    mapped = jnp.einsum("ij,kjm->kim", gram_full, path, precision=highest)
    terms = jnp.einsum("kji,kjm->kim", path, mapped, precision=highest)
    lower_factor, lower_inverse = cholesky_batch(gram_full[None], True)
    for level_index in range(levels):
        upper = terms[level_index:]
        received_terms = from_partner(upper, "leaf", level_index)
        if level_index == 1:
            lower_factor, lower_inverse, received_terms = lax.optimization_barrier(
                (lower_factor, lower_inverse, received_terms)
            )
        upper = upper + received_terms
        terms = jnp.concatenate([terms[:level_index], upper], axis=0) if level_index else upper
    scales = jnp.asarray([0.5 ** (level_index + 1) for level_index in range(levels)], jnp.float32)
    ancestor_grams = terms * scales[:, None, None]
    basis_rows = jnp.dot(sketch, lower_inverse[0].T, precision=highest)
    basis_rows, ancestor_grams = lax.optimization_barrier((basis_rows, ancestor_grams))
    returned = lax.all_to_all(
        basis_rows.astype(jnp.bfloat16), "leaf", split_axis=0, concat_axis=0, tiled=True
    )
    leaf_basis = jnp.take(returned, position, axis=0).astype(jnp.float32).T
    ancestor_factor = cholesky_batch(ancestor_grams, False)
    return (leaf_basis, lower_factor, ancestor_factor[None])


def solution(mesh):
    placed = (
        P(None, ("leaf", "blk")),
        P(("leaf", "blk"), None),
        P(),
        P("leaf", None),
        P("leaf", "blk", None),
        P(),
    )
    return jax.shard_map(
        per_device,
        mesh=mesh,
        in_specs=placed,
        out_specs=(P(None, ("leaf", "blk")), P("leaf", None, None), P("leaf", None, None, None)),
        check_vma=False,
    )
```

```python
import functools

import jax
import jax.numpy as jnp
from jax import lax
from jax.experimental import pallas as pl
from jax.experimental.pallas import tpu as pltpu
from jax.sharding import PartitionSpec as P


def from_partner(value, axis, bit):
    mask = 2**bit
    pairs = [(source, source ^ mask) for source in range(lax.axis_size(axis))]
    return lax.ppermute(value, axis, pairs)


def from_shift(value, axis, shift):
    size = lax.axis_size(axis)
    pairs = [(source, (source + shift) % size) for source in range(size)]
    return lax.ppermute(value, axis, pairs)


def kernel_tile(row_data, points):
    delta_x = row_data[0][:, None] - points[0][None, :]
    delta_y = row_data[1][:, None] - points[1][None, :]
    delta_z = row_data[2][:, None] - points[2][None, :]
    distance = delta_x * delta_x + delta_y * delta_y + delta_z * delta_z
    return (row_data[3][:, None] * lax.rsqrt(distance + 0.0009)).astype(jnp.bfloat16)


def _cholesky_body(with_inverse, a_ref, l_ref, *rest):
    if with_inverse:
        inv_ref, work, inverse_work = rest
    else:
        (work,) = rest
    count, n, _ = a_ref.shape
    rows = lax.broadcasted_iota(jnp.int32, (n, n), 0)
    cols = lax.broadcasted_iota(jnp.int32, (n, n), 1)
    work[...] = a_ref[...]
    if with_inverse:
        eye = jnp.where(rows == cols, 1.0, 0.0).astype(jnp.float32)
        for b in range(count):
            inverse_work[b] = eye
    for j in range(n):
        top = (j // 8) * 8
        sub = lax.broadcasted_iota(jnp.int32, (n - top, 1), 0) + top
        for b in range(count):
            block = work[b, top:, :]
            row = work[b, j:j + 1, :]
            pivot = row[:, j:j + 1]
            scale = lax.rsqrt(pivot)
            factor = jnp.where(sub > j, block[:, j:j + 1] * (1.0 / pivot), 0.0)
            work[b, top:, :] = jnp.where(sub == j, row * scale, block - factor * row)
            if with_inverse:
                inverse_block = inverse_work[b, top:, :]
                inverse_row = inverse_work[b, j:j + 1, :]
                inverse_work[b, top:, :] = jnp.where(
                    sub == j, inverse_row * scale, inverse_block - factor * inverse_row
                )
    for b in range(count):
        l_ref[b] = jnp.transpose(jnp.where(cols >= rows, work[b], 0.0))
        if with_inverse:
            inv_ref[b] = jnp.where(cols <= rows, inverse_work[b], 0.0)


def cholesky_batch(a, with_inverse):
    count, n, _ = a.shape
    shape = jax.ShapeDtypeStruct((count, n, n), jnp.float32)
    vmem = pl.BlockSpec(memory_space=pltpu.VMEM)
    scratch = [pltpu.VMEM((count, n, n), jnp.float32)] * (2 if with_inverse else 1)
    return pl.pallas_call(
        functools.partial(_cholesky_body, with_inverse),
        out_shape=(shape, shape) if with_inverse else shape,
        in_specs=[vmem],
        out_specs=(vmem, vmem) if with_inverse else vmem,
        scratch_shapes=scratch,
    )(a)


def per_device(panels, panel_dest, proxy_pool, proxy_index, omega, merge_maps):
    highest = lax.Precision.HIGHEST
    device_count = lax.axis_size(("leaf", "blk"))
    blk_count = lax.axis_size("blk")
    leaf_count = lax.axis_size("leaf")
    blk_index = lax.axis_index("blk")
    own_panels = panels.shape[1]
    capacity = 2 * own_panels // device_count
    rank_width = omega.shape[2]
    identity = jnp.eye(rank_width, dtype=jnp.float32)
    omega_parts = [omega[0]] + [from_shift(omega[0], "blk", shift) for shift in range(1, blk_count)]
    destination = panel_dest[:, 0] // blk_count
    capacity = blk_count * capacity
    one_hot = (destination[:, None] == jnp.arange(device_count, dtype=jnp.int32)[None, :]).astype(
        jnp.int32
    )
    running = jnp.cumsum(one_hot, axis=0)
    slot_index = jnp.sum(running * one_hot, axis=1) - 1
    position = destination * capacity + slot_index
    outgoing = jnp.zeros((4, leaf_count * capacity), jnp.float32).at[:, position].set(panels)
    outgoing = jnp.transpose(outgoing.reshape(4, leaf_count, capacity), (1, 0, 2))
    received = lax.all_to_all(outgoing, "leaf", split_axis=0, concat_axis=0, tiled=True)
    received = jnp.transpose(received, (1, 0, 2)).reshape(4, leaf_count * capacity)
    chunk = omega.shape[1]
    leaf_proxies = jnp.concatenate(
        [
            lax.dynamic_slice_in_dim(proxy_index[0], ((blk_index - shift) % blk_count) * chunk, chunk)
            for shift in range(blk_count)
        ]
    )
    points = jnp.take(proxy_pool, leaf_proxies, axis=1)
    tile = kernel_tile(received, points)
    sketch = jnp.dot(tile, jnp.concatenate(omega_parts, axis=0), preferred_element_type=jnp.float32)
    leaf_index = lax.axis_index("leaf")
    levels = leaf_count.bit_length() - 1
    path = []
    for level_index in range(levels):
        heap_index = (leaf_count >> level_index) + (leaf_index >> level_index)
        node_map = lax.dynamic_index_in_dim(merge_maps, heap_index - 2, 0, keepdims=False)
        path.append(node_map if not path else jnp.dot(path[-1], node_map, precision=highest))
    path = jnp.stack(path, axis=0)
    gram_part = jnp.dot(sketch.T, sketch, precision=highest)
    gram_sum = gram_part + from_partner(gram_part, "blk", 0)
    gram_sum = gram_sum + from_partner(gram_sum, "blk", 1)
    gram_full = gram_sum / (own_panels * blk_count) + identity
    mapped = jnp.einsum("ij,kjm->kim", gram_full, path, precision=highest)
    terms = jnp.einsum("kji,kjm->kim", path, mapped, precision=highest)
    lower_factor, lower_inverse = cholesky_batch(gram_full[None], True)
    for level_index in range(levels):
        upper = terms[level_index:]
        if level_index == levels - 1:
            basis_rows = jnp.dot(sketch, lower_inverse[0].T, precision=highest)
            basis_rows, upper = lax.optimization_barrier((basis_rows, upper))
        received_terms = from_partner(upper, "leaf", level_index)
        if level_index == 1:
            lower_factor, lower_inverse, received_terms = lax.optimization_barrier(
                (lower_factor, lower_inverse, received_terms)
            )
        upper = upper + received_terms
        terms = jnp.concatenate([terms[:level_index], upper], axis=0) if level_index else upper
    scales = jnp.asarray([0.5 ** (level_index + 1) for level_index in range(levels)], jnp.float32)
    ancestor_grams = terms * scales[:, None, None]
    returned = lax.all_to_all(
        basis_rows.astype(jnp.bfloat16), "leaf", split_axis=0, concat_axis=0, tiled=True
    )
    leaf_basis = jnp.take(returned, position, axis=0).astype(jnp.float32).T
    ancestor_factor = cholesky_batch(ancestor_grams, False)
    return (leaf_basis, lower_factor, ancestor_factor[None])


def solution(mesh):
    placed = (
        P(None, ("leaf", "blk")),
        P(("leaf", "blk"), None),
        P(),
        P("leaf", None),
        P("leaf", "blk", None),
        P(),
    )
    return jax.shard_map(
        per_device,
        mesh=mesh,
        in_specs=placed,
        out_specs=(P(None, ("leaf", "blk")), P("leaf", None, None), P("leaf", None, None, None)),
        check_vma=False,
    )
```
